128 devices in a mesh: req: 16 (over y, x), kv: 8 (over z, core).
Axes of the slice: x: 4, y: 4, z: 4, core: 2. Of those that a mesh axis runs over, the one named last changes fastest.
Arguments:
- residual: bfloat16 [16384, 2560], P(('req', 'kv')), may hold values from -6 to 6
- queries: bfloat16 [16384, 2560], P(('req', 'kv')), may hold values from -180 to 180
- suffix_kv: bfloat16 [16384, 1280], P(('req', 'kv')), may hold values from -6 to 6
- prefix_kv: bfloat16 [64, 128, 1280], P('kv'), may hold values from -6 to 6
- page_table: int32 [64], P('kv'), may hold values from 0 to 63, each once
- suffix_lens: int32 [16, 4], P('req'), may hold values from 1 to 512, 1024 in all within a row
- w_out: bfloat16 [2560, 2560], replicated, may hold values from -0.125 to 0.125
- norm_gain: float32 [2560], replicated, may hold values from 0.1 to 1.9
- w_gate: bfloat16 [2560, 7168], P(None, 'req'), may hold values from -0.125 to 0.125
- w_up: bfloat16 [2560, 7168], P(None, 'req'), may hold values from -0.125 to 0.125
- w_down: bfloat16 [7168, 2560], P('req'), may hold values from -0.0625 to 0.0625
Outputs:
- attended: bfloat16 [16384, 2560], P(('req', 'kv'))
- layer_out: bfloat16 [16384, 2560], P(('req', 'kv'))
The draws below stay inside these ranges and needn't reach their ends.
Inputs may be any that keep to these rules, and one draw needn't show every extreme that they name: `page_table`: each logical page number appears once. `suffix_lens`: each group's lengths sum to 1024.
All inputs are finite; a program needn't handle non-finite values.
Results may differ from the reference program's by a relative error of at most 0.02.
Values may be sent and summed in bfloat16 or wider, within the bound.
No kernel may reach another device: no remote copies, remote signals or barrier semaphores. Data moves between devices by JAX's collectives and lax.ppermute only.
A program may use at most 192 MiB of HBM per device.

```python
import math
import jax
import jax.numpy as jnp
import numpy as np
from jax import lax

D = 2560
QH = 32
KVH = 8
HD = 80
FF = 7168
PREFIX = 8192
PAGE = 128
REQS = 4
PAGES = 64
GROUP_TOK = 1024
MOST_LEN = 512
TOKENS = 16384
N_REQ = 16


def draw_queries(key, part):
    first_key = jax.random.fold_in(key, 11)
    values = jnp.clip(jax.random.normal(first_key, (TOKENS, QH * HD), jnp.float32) * 2.5, -15.0, 15.0)
    return values.astype(jnp.bfloat16)


def shard_levels(own_key, shape, shards, least, top_value):
    gain = 1.0
    for dim, shards_of in shards:
        steps = jax.random.uniform(jax.random.fold_in(jax.random.fold_in(own_key, 6), dim), (shards_of,), jnp.float32, least / len(shards), top_value / len(shards))
        gain = gain * jnp.repeat(jnp.exp(steps), shape[dim] // shards_of).reshape((-1,) + (1,) * (len(shape) - 1 - dim))
    return gain


def length_profile(number_of, total, limit, skew):
    loads = [(1 << 20) // math.isqrt(standing ** skew) + 1 for standing in range(2, number_of + 1)]
    spare, counts = total - limit - (number_of - 1), [1] * (number_of - 1)
    while spare > 0:
        free = [i for i in range(number_of - 1) if counts[i] < limit]
        whole, budget = sum([loads[i] for i in free]), spare
        for i in free:
            more = min(limit - counts[i], max(1, budget * loads[i] // whole), spare)
            counts[i] = counts[i] + more
            spare = spare - more
    return np.array([limit] + counts)


def ragged_sizes(stream_key, count, total, limit, slope):
    if count == 2:
        one = jax.random.randint(stream_key, (), max(1, total - limit), min(limit, total - 1) + 1)
        return jnp.stack([one, total - one])
    tallies = jnp.asarray(length_profile(count, total, limit, slope), jnp.int32)
    couples = (count - 1) // 2
    giver, receiver = tallies[1:1 + 2 * couples:2], tallies[2:2 + 2 * couples:2]
    room = jnp.minimum(giver - 1, limit - receiver)
    moved = jax.random.randint(jax.random.fold_in(stream_key, 1), (couples,), 0, 1 << 20) % (room + 1)
    tallies = tallies.at[1:1 + 2 * couples:2].set(giver - moved).at[2:2 + 2 * couples:2].set(receiver + moved)
    return tallies[jax.random.permutation(jax.random.fold_in(stream_key, 2), count)]


def centred(rng, shape, scale, limit, cuts=(), kind=jnp.bfloat16):
    result = jax.random.normal(rng, shape, jnp.float32) * scale
    if len(cuts) > 0:
        result = shard_levels(rng, shape, cuts, -0.22, 0.18) * result
    return jnp.clip(result, min=-limit, max=limit).astype(kind)


def setup_inputs(seed: int = 0) -> dict:
    keys = jax.random.split(jax.random.key(seed), 12)
    residual = centred(keys[0], (TOKENS, D), 1.0, 6.0, ((0, 128),))
    queries = draw_queries(jax.random.fold_in(keys[11], 71), 0)
    suffix_kv = centred(keys[2], (TOKENS, 2 * KVH * HD), 1.0, 6.0, ((0, 128),))
    prefix_kv = centred(keys[3], (PAGES, PAGE, 2 * KVH * HD), 1.0, 6.0, ((0, 8),))
    page_table = jax.random.permutation(keys[4], PAGES).astype(jnp.int32)
    suffix_lens = jax.vmap(lambda own: ragged_sizes(own, REQS, GROUP_TOK, MOST_LEN, 2))(jax.random.split(keys[5], N_REQ)).reshape((N_REQ, REQS)).astype(jnp.int32)
    w_out = centred(keys[6], (QH * HD, D), (QH * HD) ** -0.5, 0.125)
    norm_gain = jnp.clip(1.0 + 0.18 * jax.random.normal(keys[7], (D,), jnp.float32), 0.1, 1.9)
    w_gate = centred(keys[8], (D, FF), D ** -0.5, 0.125, ((1, 16),))
    w_up = centred(keys[9], (D, FF), D ** -0.5, 0.125, ((1, 16),))
    w_down = centred(keys[10], (FF, D), FF ** -0.5, 0.0625, ((0, 16),))
    return dict(residual=residual, queries=queries, suffix_kv=suffix_kv, prefix_kv=prefix_kv, page_table=page_table, suffix_lens=suffix_lens, w_out=w_out, norm_gain=norm_gain, w_gate=w_gate, w_up=w_up, w_down=w_down)


THETA = 1000000.0
NEG = -1e+30

def rotate(values, positions):
    half_dim = values.shape[-1] // 2
    exponent = jnp.arange(half_dim, dtype=jnp.float32) * (2.0 / values.shape[-1])
    inverse = jnp.exp(-exponent * math.log(THETA))
    angles = positions.astype(jnp.float32)[:, None] * inverse[None, :]
    cosine = jnp.cos(angles)[:, None, :]
    sine_part = jnp.sin(angles)[:, None, :]
    first_half = values[..., :half_dim]
    second = values[..., half_dim:]
    return jnp.concatenate([first_half * cosine - second * sine_part, second * cosine + first_half * sine_part], axis=-1)

def request_info(request_lens, tok_index):
    request_ends = jnp.cumsum(request_lens)
    passed = tok_index[:, None] >= request_ends[None, :]
    request_of = lax.optimization_barrier(jnp.sum(passed.astype(jnp.int32), axis=1))
    request_start = lax.optimization_barrier(jnp.sum(jnp.where(passed, request_lens[None, :], 0), axis=1))
    return (request_of, request_start)

def reference(residual, queries, suffix_kv, prefix_kv, page_table, suffix_lens, w_out, norm_gain, w_gate, w_up, w_down):
    kv_width = KVH * HD
    per_group = QH // KVH
    score_scale = HD ** (-0.5)
    page_size = prefix_kv.shape[1]
    page_pos = (page_table[:, None] * page_size + jnp.arange(page_size, dtype=jnp.int32)[None, :]).reshape(-1)
    pre_keys = rotate(prefix_kv[:, :, :kv_width].astype(jnp.float32).reshape(PREFIX, KVH, HD), page_pos).astype(jnp.bfloat16)
    pre_keys = lax.optimization_barrier(pre_keys)
    pre_values = prefix_kv[:, :, kv_width:].reshape(PREFIX, KVH, HD)
    query_len = math.gcd(GROUP_TOK, 128)

    def one_group(group_id):
        request_lens = suffix_lens[group_id]
        tok_index = jnp.arange(GROUP_TOK, dtype=jnp.int32)
        request_of, request_start = request_info(request_lens, tok_index)
        positions = PREFIX + tok_index - request_start
        q_rows = lax.dynamic_slice_in_dim(queries, group_id * GROUP_TOK, GROUP_TOK, 0)
        kv_rows = lax.dynamic_slice_in_dim(suffix_kv, group_id * GROUP_TOK, GROUP_TOK, 0)
        rotated_q = rotate(q_rows.astype(jnp.float32).reshape(GROUP_TOK, QH, HD), positions).astype(jnp.bfloat16)
        rotated_q = lax.optimization_barrier(rotated_q).reshape(GROUP_TOK, KVH, per_group, HD)
        suf_keys = rotate(kv_rows[:, :kv_width].astype(jnp.float32).reshape(GROUP_TOK, KVH, HD), positions).astype(jnp.bfloat16)
        suf_keys = lax.optimization_barrier(suf_keys)
        key_rows = jnp.concatenate([pre_keys, suf_keys], axis=0).astype(jnp.float32)
        value_rows = jnp.concatenate([pre_values, kv_rows[:, kv_width:].reshape(GROUP_TOK, KVH, HD)], axis=0).astype(jnp.float32)

        def one_block(block_id):
            query_block = lax.dynamic_slice_in_dim(rotated_q, block_id * query_len, query_len, 0).astype(jnp.float32)
            request_blk = lax.dynamic_slice_in_dim(request_of, block_id * query_len, query_len, 0)
            index_blk = lax.dynamic_slice_in_dim(tok_index, block_id * query_len, query_len, 0)
            scores = jnp.einsum('tkgd,nkd->tkgn', query_block, key_rows) * score_scale
            suffix_mask = (request_of[None, :] == request_blk[:, None]) & (tok_index[None, :] <= index_blk[:, None])
            key_mask = jnp.concatenate([jnp.ones((query_len, PREFIX), dtype=bool), suffix_mask], axis=1)
            scores = jnp.where(key_mask[:, None, None, :], scores, NEG)
            row_max = lax.optimization_barrier(jnp.max(scores, axis=-1))
            weights = jnp.where(key_mask[:, None, None, :], jnp.exp(scores - row_max[..., None]), 0.0)
            denom = lax.optimization_barrier(jnp.sum(weights, axis=-1))
            rounded = lax.optimization_barrier(weights.astype(jnp.bfloat16)).astype(jnp.float32)
            accumulated = jnp.einsum('tkgn,nkd->tkgd', rounded, value_rows)
            return (accumulated / denom[..., None]).astype(jnp.bfloat16).reshape(query_len, QH * HD)
        return lax.map(one_block, jnp.arange(GROUP_TOK // query_len, dtype=jnp.int32)).reshape(GROUP_TOK, QH * HD)
    attended = lax.map(one_group, jnp.arange(N_REQ, dtype=jnp.int32)).reshape(TOKENS, QH * HD)
    mixed_sum = residual.astype(jnp.float32) + jnp.dot(attended, w_out, preferred_element_type=jnp.float32)
    stream = lax.optimization_barrier(mixed_sum.astype(jnp.bfloat16))
    stream_wide = stream.astype(jnp.float32)
    normed = (stream_wide * lax.rsqrt(lax.optimization_barrier(jnp.mean(stream_wide * stream_wide, axis=1, keepdims=True)) + 1e-05) * norm_gain.astype(jnp.float32)).astype(jnp.bfloat16)
    shard_units = FF // N_REQ
    down_wide = w_down.astype(jnp.float32).reshape(N_REQ, shard_units, D)

    def ffn_group(group_id):
        tok_block = lax.dynamic_slice_in_dim(normed, group_id * GROUP_TOK, GROUP_TOK, 0)
        gate_proj = jnp.dot(tok_block, w_gate, preferred_element_type=jnp.float32)
        up_proj = jnp.dot(tok_block, w_up, preferred_element_type=jnp.float32)
        activated = lax.optimization_barrier((jax.nn.silu(gate_proj) * up_proj).astype(jnp.bfloat16))
        terms = jnp.einsum('tsf,sfd->tsd', activated.astype(jnp.float32).reshape(GROUP_TOK, N_REQ, shard_units), down_wide)
        terms = lax.optimization_barrier(terms.astype(jnp.bfloat16)).astype(jnp.float32)
        return lax.optimization_barrier(jnp.sum(terms, axis=1))
    summed = lax.map(ffn_group, jnp.arange(N_REQ, dtype=jnp.int32)).reshape(TOKENS, D)
    layer_out = (stream_wide + summed).astype(jnp.bfloat16)
    return (attended, layer_out)
```

```python
import math

import jax
import jax.numpy as jnp
from jax import lax
from jax.experimental import pallas as pl
from jax.experimental.pallas import tpu as pltpu
from jax.sharding import PartitionSpec as P

QH = 32
KVH = 8
HD = 80
PREFIX = 8192


THETA = 1000000.0
NEG = -1e30


def rotate(values, positions):
    half_dim = values.shape[-1] // 2
    exponent = jnp.arange(half_dim, dtype=jnp.float32) * (2.0 / values.shape[-1])
    inverse = jnp.exp(-exponent * math.log(THETA))
    angles = positions.astype(jnp.float32)[:, None] * inverse[None, :]
    cosine = jnp.cos(angles)[:, None, :]
    sine_part = jnp.sin(angles)[:, None, :]
    first_half = values[..., :half_dim]
    second = values[..., half_dim:]
    return jnp.concatenate(
        [first_half * cosine - second * sine_part, second * cosine + first_half * sine_part],
        axis=-1,
    )


def request_info(request_lens, tok_index):
    request_ends = jnp.cumsum(request_lens)
    passed = tok_index[:, None] >= request_ends[None, :]
    request_of = jnp.sum(passed.astype(jnp.int32), axis=1)
    request_start = jnp.sum(jnp.where(passed, request_lens[None, :], 0), axis=1)
    return (request_of, request_start)


def attn_kernel(q_ref, k_ref, v_ref, qi_ref, qs_ref, o_ref, *, chunks, pre_len, suf_len):
    rows = q_ref.shape[0]
    scale = HD ** (-0.5)
    q = q_ref[...]
    qi = qi_ref[...]
    qs = qs_ref[...]

    def step(j, carry):
        m, l, acc = carry
        kt = k_ref[j]
        vt = v_ref[j]
        s = jnp.dot(q, kt, preferred_element_type=jnp.float32) * scale
        kidx = j * suf_len + lax.broadcasted_iota(jnp.int32, (rows, suf_len), 1)
        mask = (kidx >= qs) & (kidx <= qi)
        s_pre = s[:, :pre_len]
        s_suf = jnp.where(mask, s[:, pre_len:], NEG)
        m_new = jnp.maximum(
            m,
            jnp.maximum(
                jnp.max(s_pre, axis=1, keepdims=True), jnp.max(s_suf, axis=1, keepdims=True)
            ),
        )
        alpha = jnp.exp(m - m_new)
        p_pre = jnp.exp(s_pre - m_new)
        p_suf = jnp.where(mask, jnp.exp(s_suf - m_new), 0.0)
        l_new = alpha * l + (
            jnp.sum(p_pre, axis=1, keepdims=True) + jnp.sum(p_suf, axis=1, keepdims=True)
        )
        p = jnp.concatenate([p_pre, p_suf], axis=1).astype(jnp.bfloat16)
        pv = lax.dot_general(
            p, vt, (((1,), (1,)), ((), ())), preferred_element_type=jnp.float32
        )
        return (m_new, l_new, alpha * acc + pv)

    init = (
        jnp.full((rows, 1), NEG, jnp.float32),
        jnp.zeros((rows, 1), jnp.float32),
        jnp.zeros((rows, HD), jnp.float32),
    )
    m, l, acc = lax.fori_loop(0, chunks, step, init)
    o_ref[...] = (acc / l).astype(o_ref.dtype)


def attention(q_heads, kv_t, qidx, qstart, pre_len, suf_len):
    heads, rows, _ = q_heads.shape
    chunks = kv_t.shape[0]
    width = kv_t.shape[2]
    kernel = lambda *refs: attn_kernel(*refs, chunks=chunks, pre_len=pre_len, suf_len=suf_len)
    return pl.pallas_call(
        kernel,
        grid=(heads,),
        in_specs=[
            pl.BlockSpec((None, rows, HD), lambda h: (h, 0, 0)),
            pl.BlockSpec((chunks, HD, width), lambda h: (0, h, 0)),
            pl.BlockSpec((chunks, HD, width), lambda h: (0, heads + h, 0)),
            pl.BlockSpec((rows, 1), lambda h: (0, 0)),
            pl.BlockSpec((rows, 1), lambda h: (0, 0)),
        ],
        out_specs=pl.BlockSpec((None, rows, HD), lambda h: (h, 0, 0)),
        out_shape=jax.ShapeDtypeStruct((heads, rows, HD), jnp.bfloat16),
        compiler_params=pltpu.CompilerParams(
            dimension_semantics=("arbitrary",), vmem_limit_bytes=48 * 1024 * 1024
        ),
    )(q_heads, kv_t, kv_t, qidx, qstart)


def body(
    residual,
    queries,
    suffix_kv,
    prefix_kv,
    page_table,
    suffix_lens,
    w_out,
    norm_gain,
    w_gate,
    w_up,
    w_down,
):
    tok_rows = queries.shape[0]
    kv_width = KVH * HD
    per_group = QH // KVH
    tok_index = lax.axis_index("kv") * tok_rows + jnp.arange(tok_rows, dtype=jnp.int32)
    request_lens = suffix_lens[0]
    request_of, request_start = request_info(request_lens, tok_index)
    positions = PREFIX + tok_index - request_start
    rotated_q = rotate(queries.astype(jnp.float32).reshape(tok_rows, QH, HD), positions).astype(
        jnp.bfloat16
    )
    q_heads = (
        rotated_q.reshape(tok_rows, KVH, per_group, HD)
        .transpose(1, 2, 0, 3)
        .reshape(KVH, per_group * tok_rows, HD)
    )
    suf_keys = rotate(
        suffix_kv[:, :kv_width].astype(jnp.float32).reshape(tok_rows, KVH, HD), positions
    ).astype(jnp.bfloat16)
    page_count = prefix_kv.shape[0]
    page_size = prefix_kv.shape[1]
    pre_len = page_count * page_size
    page_pos = (
        page_table[:, None] * page_size + jnp.arange(page_size, dtype=jnp.int32)[None, :]
    ).reshape(-1)
    page_keys = rotate(
        prefix_kv[:, :, :kv_width].astype(jnp.float32).reshape(pre_len, KVH, HD),
        page_pos,
    ).astype(jnp.bfloat16)
    keys_all = jnp.concatenate(
        [page_keys.reshape(pre_len, kv_width), suf_keys.reshape(tok_rows, kv_width)], axis=0
    )
    values_all = jnp.concatenate(
        [prefix_kv[:, :, kv_width:].reshape(pre_len, kv_width), suffix_kv[:, kv_width:]], axis=0
    )
    local_t = jnp.concatenate([keys_all, values_all], axis=1).T
    kv_t = lax.all_gather(local_t[None], "kv", axis=0, tiled=True)
    qidx = jnp.tile(tok_index, per_group)[:, None]
    qstart = jnp.tile(request_start, per_group)[:, None]
    out_heads = attention(q_heads, kv_t, qidx, qstart, pre_len, tok_rows)
    attended = (
        out_heads.reshape(KVH, per_group, tok_rows, HD)
        .transpose(2, 0, 1, 3)
        .reshape(tok_rows, QH * HD)
    )
    mixed_sum = residual.astype(jnp.float32) + jnp.dot(
        attended, w_out, preferred_element_type=jnp.float32
    )
    stream_wide = mixed_sum.astype(jnp.bfloat16).astype(jnp.float32)
    normed = (
        stream_wide
        * lax.rsqrt(jnp.mean(stream_wide * stream_wide, axis=1, keepdims=True) + 1e-05)
        * norm_gain
    ).astype(jnp.bfloat16)
    shard_piece = lax.all_gather(normed, "req", axis=0, tiled=True)
    gate_proj = jnp.dot(shard_piece, w_gate, preferred_element_type=jnp.float32)
    up_proj = jnp.dot(shard_piece, w_up, preferred_element_type=jnp.float32)
    activated = (jax.nn.silu(gate_proj) * up_proj).astype(jnp.bfloat16)
    summed = lax.psum_scatter(
        jnp.dot(activated, w_down, preferred_element_type=jnp.float32).astype(jnp.bfloat16),
        "req",
        scatter_dimension=0,
        tiled=True,
    ).astype(jnp.float32)
    layer_out = (stream_wide + summed).astype(jnp.bfloat16)
    return (attended, layer_out)


def solution(mesh):
    in_specs = (
        P(("req", "kv"), None),
        P(("req", "kv"), None),
        P(("req", "kv"), None),
        P("kv", None, None),
        P("kv"),
        P("req", None),
        P(),
        P(),
        P(None, "req"),
        P(None, "req"),
        P("req", None),
    )
    out_specs = (P(("req", "kv"), None), P(("req", "kv"), None))
    return jax.shard_map(body, mesh=mesh, in_specs=in_specs, out_specs=out_specs, check_vma=False)
```

```python
import math

import jax
import jax.numpy as jnp
from jax import lax
from jax.experimental import pallas as pl
from jax.experimental.pallas import tpu as pltpu
from jax.sharding import PartitionSpec as P

QH = 32
KVH = 8
HD = 80
PREFIX = 8192


THETA = 1000000.0
NEG = -1e30


def rotate(values, positions):
    half_dim = values.shape[-1] // 2
    exponent = jnp.arange(half_dim, dtype=jnp.float32) * (2.0 / values.shape[-1])
    inverse = jnp.exp(-exponent * math.log(THETA))
    angles = positions.astype(jnp.float32)[:, None] * inverse[None, :]
    cosine = jnp.cos(angles)[:, None, :]
    sine_part = jnp.sin(angles)[:, None, :]
    first_half = values[..., :half_dim]
    second = values[..., half_dim:]
    return jnp.concatenate(
        [first_half * cosine - second * sine_part, second * cosine + first_half * sine_part],
        axis=-1,
    )


def request_info(request_lens, tok_index):
    request_ends = jnp.cumsum(request_lens)
    passed = tok_index[:, None] >= request_ends[None, :]
    request_of = jnp.sum(passed.astype(jnp.int32), axis=1)
    request_start = jnp.sum(jnp.where(passed, request_lens[None, :], 0), axis=1)
    return (request_of, request_start)


def attn_kernel(q_ref, k_ref, v_ref, qi_ref, qs_ref, o_ref, *, chunks, pre_len, suf_len):
    rows = q_ref.shape[0]
    scale = HD ** (-0.5)
    q = q_ref[...]
    qi = qi_ref[...]
    qs = qs_ref[...]

    def step(j, carry):
        m, l, acc = carry
        kt = k_ref[j]
        vt = v_ref[j]
        s_pre = jnp.dot(q, kt[:, :pre_len], preferred_element_type=jnp.float32) * scale
        s_suf = jnp.dot(q, kt[:, pre_len:], preferred_element_type=jnp.float32) * scale
        kidx = j * suf_len + lax.broadcasted_iota(jnp.int32, (rows, suf_len), 1)
        mask = (kidx >= qs) & (kidx <= qi)
        s_suf = jnp.where(mask, s_suf, NEG)
        m_new = jnp.maximum(
            m,
            jnp.maximum(
                jnp.max(s_pre, axis=1, keepdims=True), jnp.max(s_suf, axis=1, keepdims=True)
            ),
        )
        alpha = jnp.exp(m - m_new)
        p_pre = jnp.exp(s_pre - m_new)
        p_suf = jnp.where(mask, jnp.exp(s_suf - m_new), 0.0)
        l_new = alpha * l + (
            jnp.sum(p_pre, axis=1, keepdims=True) + jnp.sum(p_suf, axis=1, keepdims=True)
        )
        nt = (((1,), (1,)), ((), ()))
        pv = lax.dot_general(
            p_pre.astype(jnp.bfloat16), vt[:, :pre_len], nt, preferred_element_type=jnp.float32
        ) + lax.dot_general(
            p_suf.astype(jnp.bfloat16), vt[:, pre_len:], nt, preferred_element_type=jnp.float32
        )
        return (m_new, l_new, alpha * acc + pv)

    init = (
        jnp.full((rows, 1), NEG, jnp.float32),
        jnp.zeros((rows, 1), jnp.float32),
        jnp.zeros((rows, HD), jnp.float32),
    )
    m, l, acc = lax.fori_loop(0, chunks, step, init)
    o_ref[...] = (acc / l).astype(o_ref.dtype)


def attention(q_heads, kv_t, qidx, qstart, pre_len, suf_len):
    heads, rows, _ = q_heads.shape
    chunks = kv_t.shape[0]
    width = kv_t.shape[2]
    kernel = lambda *refs: attn_kernel(*refs, chunks=chunks, pre_len=pre_len, suf_len=suf_len)
    return pl.pallas_call(
        kernel,
        grid=(heads,),
        in_specs=[
            pl.BlockSpec((None, rows, HD), lambda h: (h, 0, 0)),
            pl.BlockSpec((chunks, HD, width), lambda h: (0, h, 0)),
            pl.BlockSpec((chunks, HD, width), lambda h: (0, heads + h, 0)),
            pl.BlockSpec((rows, 1), lambda h: (0, 0)),
            pl.BlockSpec((rows, 1), lambda h: (0, 0)),
        ],
        out_specs=pl.BlockSpec((None, rows, HD), lambda h: (h, 0, 0)),
        out_shape=jax.ShapeDtypeStruct((heads, rows, HD), jnp.bfloat16),
        compiler_params=pltpu.CompilerParams(
            dimension_semantics=("arbitrary",), vmem_limit_bytes=48 * 1024 * 1024
        ),
    )(q_heads, kv_t, kv_t, qidx, qstart)


def body(
    residual,
    queries,
    suffix_kv,
    prefix_kv,
    page_table,
    suffix_lens,
    w_out,
    norm_gain,
    w_gate,
    w_up,
    w_down,
):
    tok_rows = queries.shape[0]
    kv_width = KVH * HD
    per_group = QH // KVH
    tok_index = lax.axis_index("kv") * tok_rows + jnp.arange(tok_rows, dtype=jnp.int32)
    request_lens = suffix_lens[0]
    request_of, request_start = request_info(request_lens, tok_index)
    positions = PREFIX + tok_index - request_start
    rotated_q = rotate(queries.astype(jnp.float32).reshape(tok_rows, QH, HD), positions).astype(
        jnp.bfloat16
    )
    q_heads = (
        rotated_q.reshape(tok_rows, KVH, per_group, HD)
        .transpose(1, 2, 0, 3)
        .reshape(KVH, per_group * tok_rows, HD)
    )
    suf_keys = rotate(
        suffix_kv[:, :kv_width].astype(jnp.float32).reshape(tok_rows, KVH, HD), positions
    ).astype(jnp.bfloat16)
    page_count = prefix_kv.shape[0]
    page_size = prefix_kv.shape[1]
    pre_len = page_count * page_size
    page_pos = (
        page_table[:, None] * page_size + jnp.arange(page_size, dtype=jnp.int32)[None, :]
    ).reshape(-1)
    page_keys = rotate(
        prefix_kv[:, :, :kv_width].astype(jnp.float32).reshape(pre_len, KVH, HD),
        page_pos,
    ).astype(jnp.bfloat16)
    keys_all = jnp.concatenate(
        [page_keys.reshape(pre_len, kv_width), suf_keys.reshape(tok_rows, kv_width)], axis=0
    )
    values_all = jnp.concatenate(
        [prefix_kv[:, :, kv_width:].reshape(pre_len, kv_width), suffix_kv[:, kv_width:]], axis=0
    )
    n_chunks = 4
    chunk_heads = KVH // n_chunks
    chunk_rows = chunk_heads * HD
    keys_t = keys_all.T.reshape(n_chunks, chunk_rows, pre_len + tok_rows)
    values_t = values_all.T.reshape(n_chunks, chunk_rows, pre_len + tok_rows)
    local_t = jnp.concatenate([keys_t, values_t], axis=1)
    qidx = jnp.tile(tok_index, per_group)[:, None]
    qstart = jnp.tile(request_start, per_group)[:, None]
    outs = []
    for c in range(n_chunks):
        kv_t = lax.all_gather(local_t[c][None], "kv", axis=0, tiled=True)
        outs.append(
            attention(
                q_heads[c * chunk_heads:(c + 1) * chunk_heads], kv_t, qidx, qstart, pre_len, tok_rows
            )
        )
    out_heads = jnp.concatenate(outs, axis=0)
    attended = (
        out_heads.reshape(KVH, per_group, tok_rows, HD)
        .transpose(2, 0, 1, 3)
        .reshape(tok_rows, QH * HD)
    )
    mixed_sum = residual.astype(jnp.float32) + jnp.dot(
        attended, w_out, preferred_element_type=jnp.float32
    )
    stream_wide = mixed_sum.astype(jnp.bfloat16).astype(jnp.float32)
    normed = (
        stream_wide
        * lax.rsqrt(jnp.mean(stream_wide * stream_wide, axis=1, keepdims=True) + 1e-05)
        * norm_gain
    ).astype(jnp.bfloat16)
    shard_piece = lax.all_gather(normed, "req", axis=0, tiled=True)
    gate_proj = jnp.dot(shard_piece, w_gate, preferred_element_type=jnp.float32)
    up_proj = jnp.dot(shard_piece, w_up, preferred_element_type=jnp.float32)
    activated = (jax.nn.silu(gate_proj) * up_proj).astype(jnp.bfloat16)
    summed = lax.psum_scatter(
        jnp.dot(activated, w_down, preferred_element_type=jnp.float32).astype(jnp.bfloat16),
        "req",
        scatter_dimension=0,
        tiled=True,
    ).astype(jnp.float32)
    layer_out = (stream_wide + summed).astype(jnp.bfloat16)
    return (attended, layer_out)


def solution(mesh):
    in_specs = (
        P(("req", "kv"), None),
        P(("req", "kv"), None),
        P(("req", "kv"), None),
        P("kv", None, None),
        P("kv"),
        P("req", None),
        P(),
        P(),
        P(None, "req"),
        P(None, "req"),
        P("req", None),
    )
    out_specs = (P(("req", "kv"), None), P(("req", "kv"), None))
    return jax.shard_map(body, mesh=mesh, in_specs=in_specs, out_specs=out_specs, check_vma=False)
```

```python
import math

import jax
import jax.numpy as jnp
from jax import lax
from jax.experimental import pallas as pl
from jax.experimental.pallas import tpu as pltpu
from jax.sharding import PartitionSpec as P

QH = 32
KVH = 8
HD = 80
PREFIX = 8192


THETA = 1000000.0
NEG = -1e30


def rotate(values, positions):
    half_dim = values.shape[-1] // 2
    exponent = jnp.arange(half_dim, dtype=jnp.float32) * (2.0 / values.shape[-1])
    inverse = jnp.exp(-exponent * math.log(THETA))
    angles = positions.astype(jnp.float32)[:, None] * inverse[None, :]
    cosine = jnp.cos(angles)[:, None, :]
    sine_part = jnp.sin(angles)[:, None, :]
    first_half = values[..., :half_dim]
    second = values[..., half_dim:]
    return jnp.concatenate(
        [first_half * cosine - second * sine_part, second * cosine + first_half * sine_part],
        axis=-1,
    )


def request_info(request_lens, tok_index):
    request_ends = jnp.cumsum(request_lens)
    passed = tok_index[:, None] >= request_ends[None, :]
    request_of = jnp.sum(passed.astype(jnp.int32), axis=1)
    request_start = jnp.sum(jnp.where(passed, request_lens[None, :], 0), axis=1)
    return (request_of, request_start)


def attn_kernel(q_ref, k_ref, v_ref, qi_ref, qs_ref, o_ref, *, chunks, pre_len, suf_len):
    rows = q_ref.shape[0]
    scale = HD ** (-0.5)
    q = q_ref[...]
    qi = qi_ref[...]
    qs = qs_ref[...]

    def step(j, carry):
        m, l, acc = carry
        kt = k_ref[j]
        vt = v_ref[j]
        s_pre = jnp.dot(q, kt[:, :pre_len], preferred_element_type=jnp.float32) * scale
        s_suf = jnp.dot(q, kt[:, pre_len:], preferred_element_type=jnp.float32) * scale
        kidx = j * suf_len + lax.broadcasted_iota(jnp.int32, (rows, suf_len), 1)
        mask = (kidx >= qs) & (kidx <= qi)
        s_suf = jnp.where(mask, s_suf, NEG)
        m_new = jnp.maximum(
            m,
            jnp.maximum(
                jnp.max(s_pre, axis=1, keepdims=True), jnp.max(s_suf, axis=1, keepdims=True)
            ),
        )
        alpha = jnp.exp(m - m_new)
        p_pre = jnp.exp(s_pre - m_new)
        p_suf = jnp.where(mask, jnp.exp(s_suf - m_new), 0.0)
        l_new = alpha * l + (
            jnp.sum(p_pre, axis=1, keepdims=True) + jnp.sum(p_suf, axis=1, keepdims=True)
        )
        nt = (((1,), (1,)), ((), ()))
        pv = lax.dot_general(
            p_pre.astype(jnp.bfloat16), vt[:, :pre_len], nt, preferred_element_type=jnp.float32
        ) + lax.dot_general(
            p_suf.astype(jnp.bfloat16), vt[:, pre_len:], nt, preferred_element_type=jnp.float32
        )
        return (m_new, l_new, alpha * acc + pv)

    init = (
        jnp.full((rows, 1), NEG, jnp.float32),
        jnp.zeros((rows, 1), jnp.float32),
        jnp.zeros((rows, HD), jnp.float32),
    )
    m, l, acc = lax.fori_loop(0, chunks, step, init)
    o_ref[...] = (acc / l).astype(o_ref.dtype)


def attention(q_heads, kv_t, qidx, qstart, pre_len, suf_len):
    heads, rows, _ = q_heads.shape
    chunks = kv_t.shape[0]
    width = kv_t.shape[2]
    kernel = lambda *refs: attn_kernel(*refs, chunks=chunks, pre_len=pre_len, suf_len=suf_len)
    return pl.pallas_call(
        kernel,
        grid=(heads,),
        in_specs=[
            pl.BlockSpec((None, rows, HD), lambda h: (h, 0, 0)),
            pl.BlockSpec((chunks, HD, width), lambda h: (0, h, 0)),
            pl.BlockSpec((chunks, HD, width), lambda h: (0, heads + h, 0)),
            pl.BlockSpec((rows, 1), lambda h: (0, 0)),
            pl.BlockSpec((rows, 1), lambda h: (0, 0)),
        ],
        out_specs=pl.BlockSpec((None, rows, HD), lambda h: (h, 0, 0)),
        out_shape=jax.ShapeDtypeStruct((heads, rows, HD), jnp.bfloat16),
        compiler_params=pltpu.CompilerParams(
            dimension_semantics=("arbitrary",), vmem_limit_bytes=48 * 1024 * 1024
        ),
    )(q_heads, kv_t, kv_t, qidx, qstart)


def body(
    residual,
    queries,
    suffix_kv,
    prefix_kv,
    page_table,
    suffix_lens,
    w_out,
    norm_gain,
    w_gate,
    w_up,
    w_down,
):
    tok_rows = queries.shape[0]
    kv_width = KVH * HD
    per_group = QH // KVH
    tok_index = lax.axis_index("kv") * tok_rows + jnp.arange(tok_rows, dtype=jnp.int32)
    request_lens = suffix_lens[0]
    request_of, request_start = request_info(request_lens, tok_index)
    positions = PREFIX + tok_index - request_start
    rotated_q = rotate(queries.astype(jnp.float32).reshape(tok_rows, QH, HD), positions).astype(
        jnp.bfloat16
    )
    q_heads = (
        rotated_q.reshape(tok_rows, KVH, per_group, HD)
        .transpose(1, 2, 0, 3)
        .reshape(KVH, per_group * tok_rows, HD)
    )
    page_count = prefix_kv.shape[0]
    page_size = prefix_kv.shape[1]
    pre_len = page_count * page_size
    key_count = pre_len + tok_rows
    page_pos = (
        page_table[:, None] * page_size + jnp.arange(page_size, dtype=jnp.int32)[None, :]
    ).reshape(-1)
    key_pos = jnp.concatenate([page_pos, positions]).astype(jnp.float32)
    raw_t = jnp.concatenate(
        [prefix_kv.reshape(pre_len, 2 * kv_width), suffix_kv], axis=0
    ).T
    half_dim = HD // 2
    exponent = jnp.arange(half_dim, dtype=jnp.float32) * (2.0 / HD)
    inverse = jnp.exp(-exponent * math.log(THETA))
    angles = inverse[:, None] * key_pos[None, :]
    cosine = jnp.cos(angles)[None]
    sine_part = jnp.sin(angles)[None]
    halves = raw_t[:kv_width].astype(jnp.float32).reshape(KVH, 2, half_dim, key_count)
    first_half = halves[:, 0]
    second = halves[:, 1]
    keys_t = jnp.stack(
        [first_half * cosine - second * sine_part, second * cosine + first_half * sine_part],
        axis=1,
    ).astype(jnp.bfloat16)
    values_t = raw_t[kv_width:]
    n_chunks = 4
    chunk_heads = KVH // n_chunks
    chunk_rows = chunk_heads * HD
    local_t = jnp.concatenate(
        [
            keys_t.reshape(n_chunks, chunk_rows, key_count),
            values_t.reshape(n_chunks, chunk_rows, key_count),
        ],
        axis=1,
    )
    qidx = jnp.tile(tok_index, per_group)[:, None]
    qstart = jnp.tile(request_start, per_group)[:, None]
    pieces = []
    mixed_sum = residual.astype(jnp.float32)
    for c in range(n_chunks):
        kv_t = lax.all_gather(local_t[c][None], "kv", axis=0, tiled=True)
        out_c = attention(
            q_heads[c * chunk_heads:(c + 1) * chunk_heads], kv_t, qidx, qstart, pre_len, tok_rows
        )
        piece = (
            out_c.reshape(chunk_heads, per_group, tok_rows, HD)
            .transpose(2, 0, 1, 3)
            .reshape(tok_rows, chunk_heads * per_group * HD)
        )
        width = piece.shape[1]
        mixed_sum = mixed_sum + jnp.dot(
            piece, w_out[c * width:(c + 1) * width], preferred_element_type=jnp.float32
        )
        pieces.append(piece)
    attended = jnp.concatenate(pieces, axis=1)
    stream_wide = mixed_sum.astype(jnp.bfloat16).astype(jnp.float32)
    normed = (
        stream_wide
        * lax.rsqrt(jnp.mean(stream_wide * stream_wide, axis=1, keepdims=True) + 1e-05)
        * norm_gain
    ).astype(jnp.bfloat16)
    shard_piece = lax.all_gather(normed, "req", axis=0, tiled=True)
    gate_proj = jnp.dot(shard_piece, w_gate, preferred_element_type=jnp.float32)
    up_proj = jnp.dot(shard_piece, w_up, preferred_element_type=jnp.float32)
    activated = (jax.nn.silu(gate_proj) * up_proj).astype(jnp.bfloat16)
    summed = lax.psum_scatter(
        jnp.dot(activated, w_down, preferred_element_type=jnp.float32).astype(jnp.bfloat16),
        "req",
        scatter_dimension=0,
        tiled=True,
    ).astype(jnp.float32)
    layer_out = (stream_wide + summed).astype(jnp.bfloat16)
    return (attended, layer_out)


def solution(mesh):
    in_specs = (
        P(("req", "kv"), None),
        P(("req", "kv"), None),
        P(("req", "kv"), None),
        P("kv", None, None),
        P("kv"),
        P("req", None),
        P(),
        P(),
        P(None, "req"),
        P(None, "req"),
        P("req", None),
    )
    out_specs = (P(("req", "kv"), None), P(("req", "kv"), None))
    return jax.shard_map(body, mesh=mesh, in_specs=in_specs, out_specs=out_specs, check_vma=False)
```

```python
import math

import jax
import jax.numpy as jnp
from jax import lax
from jax.experimental import pallas as pl
from jax.experimental.pallas import tpu as pltpu
from jax.sharding import PartitionSpec as P

QH = 32
KVH = 8
HD = 80
PREFIX = 8192


THETA = 1000000.0
NEG = -1e30


def rotate(values, positions):
    half_dim = values.shape[-1] // 2
    exponent = jnp.arange(half_dim, dtype=jnp.float32) * (2.0 / values.shape[-1])
    inverse = jnp.exp(-exponent * math.log(THETA))
    angles = positions.astype(jnp.float32)[:, None] * inverse[None, :]
    cosine = jnp.cos(angles)[:, None, :]
    sine_part = jnp.sin(angles)[:, None, :]
    first_half = values[..., :half_dim]
    second = values[..., half_dim:]
    return jnp.concatenate(
        [first_half * cosine - second * sine_part, second * cosine + first_half * sine_part],
        axis=-1,
    )


def request_info(request_lens, tok_index):
    request_ends = jnp.cumsum(request_lens)
    passed = tok_index[:, None] >= request_ends[None, :]
    request_of = jnp.sum(passed.astype(jnp.int32), axis=1)
    request_start = jnp.sum(jnp.where(passed, request_lens[None, :], 0), axis=1)
    return (request_of, request_start)


def attn_kernel(q_ref, k_ref, v_ref, qi_ref, qs_ref, m_in, l_in, acc_in, m_ref, l_ref, acc_ref, *, pre_len):
    rows = q_ref.shape[0]
    suf_len = k_ref.shape[1] - pre_len
    scale = HD ** (-0.5)
    q = q_ref[...]
    kt = k_ref[...]
    vt = v_ref[...]
    m = m_in[...]
    l = l_in[...]
    s_pre = jnp.dot(q, kt[:, :pre_len], preferred_element_type=jnp.float32) * scale
    s_suf = jnp.dot(q, kt[:, pre_len:], preferred_element_type=jnp.float32) * scale
    kidx = lax.broadcasted_iota(jnp.int32, (rows, suf_len), 1)
    mask = (kidx >= qs_ref[...]) & (kidx <= qi_ref[...])
    s_suf = jnp.where(mask, s_suf, NEG)
    m_new = jnp.maximum(
        m,
        jnp.maximum(jnp.max(s_pre, axis=1, keepdims=True), jnp.max(s_suf, axis=1, keepdims=True)),
    )
    alpha = jnp.exp(m - m_new)
    p_pre = jnp.exp(s_pre - m_new)
    p_suf = jnp.where(mask, jnp.exp(s_suf - m_new), 0.0)
    l_ref[...] = alpha * l + (
        jnp.sum(p_pre, axis=1, keepdims=True) + jnp.sum(p_suf, axis=1, keepdims=True)
    )
    nt = (((1,), (1,)), ((), ()))
    pv = lax.dot_general(
        p_pre.astype(jnp.bfloat16), vt[:, :pre_len], nt, preferred_element_type=jnp.float32
    ) + lax.dot_general(
        p_suf.astype(jnp.bfloat16), vt[:, pre_len:], nt, preferred_element_type=jnp.float32
    )
    acc_ref[...] = alpha * acc_in[...] + pv
    m_ref[...] = m_new


def attention_block(q_heads, kv_blk, qi_rel, qs_rel, state, pre_len):
    heads, rows, _ = q_heads.shape
    width = kv_blk.shape[1]
    m, l, acc = state
    kernel = lambda *refs: attn_kernel(*refs, pre_len=pre_len)
    stat_spec = pl.BlockSpec((None, rows, 1), lambda h: (h, 0, 0))
    acc_spec = pl.BlockSpec((None, rows, HD), lambda h: (h, 0, 0))
    return pl.pallas_call(
        kernel,
        grid=(heads,),
        in_specs=[
            pl.BlockSpec((None, rows, HD), lambda h: (h, 0, 0)),
            pl.BlockSpec((HD, width), lambda h: (h, 0)),
            pl.BlockSpec((HD, width), lambda h: (heads + h, 0)),
            pl.BlockSpec((rows, 1), lambda h: (0, 0)),
            pl.BlockSpec((rows, 1), lambda h: (0, 0)),
            stat_spec,
            stat_spec,
            acc_spec,
        ],
        out_specs=[stat_spec, stat_spec, acc_spec],
        out_shape=[
            jax.ShapeDtypeStruct(m.shape, jnp.float32),
            jax.ShapeDtypeStruct(l.shape, jnp.float32),
            jax.ShapeDtypeStruct(acc.shape, jnp.float32),
        ],
        input_output_aliases={5: 0, 6: 1, 7: 2},
        cost_estimate=pl.CostEstimate(
            flops=4 * heads * rows * width * HD,
            transcendentals=heads * rows * width,
            bytes_accessed=2 * kv_blk.size + 4 * acc.size,
        ),
        compiler_params=pltpu.CompilerParams(
            dimension_semantics=("arbitrary",), vmem_limit_bytes=48 * 1024 * 1024
        ),
    )(q_heads, kv_blk, kv_blk, qi_rel, qs_rel, m, l, acc)


def body(
    residual,
    queries,
    suffix_kv,
    prefix_kv,
    page_table,
    suffix_lens,
    w_out,
    norm_gain,
    w_gate,
    w_up,
    w_down,
):
    tok_rows = queries.shape[0]
    kv_width = KVH * HD
    per_group = QH // KVH
    tok_index = lax.axis_index("kv") * tok_rows + jnp.arange(tok_rows, dtype=jnp.int32)
    request_lens = suffix_lens[0]
    request_of, request_start = request_info(request_lens, tok_index)
    positions = PREFIX + tok_index - request_start
    rotated_q = rotate(queries.astype(jnp.float32).reshape(tok_rows, QH, HD), positions).astype(
        jnp.bfloat16
    )
    q_heads = (
        rotated_q.reshape(tok_rows, KVH, per_group, HD)
        .transpose(1, 2, 0, 3)
        .reshape(KVH, per_group * tok_rows, HD)
    )
    page_count = prefix_kv.shape[0]
    page_size = prefix_kv.shape[1]
    pre_len = page_count * page_size
    key_count = pre_len + tok_rows
    page_pos = (
        page_table[:, None] * page_size + jnp.arange(page_size, dtype=jnp.int32)[None, :]
    ).reshape(-1)
    key_pos = jnp.concatenate([page_pos, positions]).astype(jnp.float32)
    raw_t = jnp.concatenate(
        [prefix_kv.reshape(pre_len, 2 * kv_width), suffix_kv], axis=0
    ).T
    half_dim = HD // 2
    exponent = jnp.arange(half_dim, dtype=jnp.float32) * (2.0 / HD)
    inverse = jnp.exp(-exponent * math.log(THETA))
    angles = inverse[:, None] * key_pos[None, :]
    cosine = jnp.cos(angles)[None]
    sine_part = jnp.sin(angles)[None]
    halves = raw_t[:kv_width].astype(jnp.float32).reshape(KVH, 2, half_dim, key_count)
    first_half = halves[:, 0]
    second = halves[:, 1]
    keys_t = jnp.stack(
        [first_half * cosine - second * sine_part, second * cosine + first_half * sine_part],
        axis=1,
    ).astype(jnp.bfloat16)
    values_t = raw_t[kv_width:]
    local_t = jnp.concatenate([keys_t.reshape(kv_width, key_count), values_t], axis=0)
    qidx = jnp.tile(tok_index, per_group)[:, None]
    qstart = jnp.tile(request_start, per_group)[:, None]
    rows = per_group * tok_rows
    state = (
        jnp.full((KVH, rows, 1), NEG, jnp.float32),
        jnp.zeros((KVH, rows, 1), jnp.float32),
        jnp.zeros((KVH, rows, HD), jnp.float32),
    )
    n_kv = lax.axis_size("kv")
    me = lax.axis_index("kv")

    def absorb_block(state, blk, owner):
        return attention_block(
            q_heads, blk, qidx - owner * tok_rows, qstart - owner * tok_rows, state, pre_len
        )

    cw_pairs = [(i, (i + 1) % n_kv) for i in range(n_kv)]
    ccw_pairs = [(i, (i - 1) % n_kv) for i in range(n_kv)]
    prev_state = state
    state = absorb_block(state, local_t, me)
    cw_blk = local_t
    ccw_blk = local_t
    for step in range(1, n_kv // 2 + 1):
        if step > 1:
            (cw_blk, ccw_blk), unused = lax.optimization_barrier(((cw_blk, ccw_blk), prev_state))
        prev_state = state
        cw_blk = lax.ppermute(cw_blk, "kv", cw_pairs)
        if step < n_kv - step:
            ccw_blk = lax.ppermute(ccw_blk, "kv", ccw_pairs)
        state = absorb_block(state, cw_blk, (me - step) % n_kv)
        if step < n_kv - step:
            state = absorb_block(state, ccw_blk, (me + step) % n_kv)
    final_max, denom, accumulated = state
    out_heads = (accumulated / denom).astype(jnp.bfloat16)
    attended = (
        out_heads.reshape(KVH, per_group, tok_rows, HD)
        .transpose(2, 0, 1, 3)
        .reshape(tok_rows, QH * HD)
    )
    mixed_sum = residual.astype(jnp.float32) + jnp.dot(
        attended, w_out, preferred_element_type=jnp.float32
    )
    stream_wide = mixed_sum.astype(jnp.bfloat16).astype(jnp.float32)
    normed = (
        stream_wide
        * lax.rsqrt(jnp.mean(stream_wide * stream_wide, axis=1, keepdims=True) + 1e-05)
        * norm_gain
    ).astype(jnp.bfloat16)
    shard_piece = lax.all_gather(normed, "req", axis=0, tiled=True)
    gate_proj = jnp.dot(shard_piece, w_gate, preferred_element_type=jnp.float32)
    up_proj = jnp.dot(shard_piece, w_up, preferred_element_type=jnp.float32)
    activated = (jax.nn.silu(gate_proj) * up_proj).astype(jnp.bfloat16)
    summed = lax.psum_scatter(
        jnp.dot(activated, w_down, preferred_element_type=jnp.float32).astype(jnp.bfloat16),
        "req",
        scatter_dimension=0,
        tiled=True,
    ).astype(jnp.float32)
    layer_out = (stream_wide + summed).astype(jnp.bfloat16)
    return (attended, layer_out)


def solution(mesh):
    in_specs = (
        P(("req", "kv"), None),
        P(("req", "kv"), None),
        P(("req", "kv"), None),
        P("kv", None, None),
        P("kv"),
        P("req", None),
        P(),
        P(),
        P(None, "req"),
        P(None, "req"),
        P("req", None),
    )
    out_specs = (P(("req", "kv"), None), P(("req", "kv"), None))
    return jax.shard_map(body, mesh=mesh, in_specs=in_specs, out_specs=out_specs, check_vma=False)
```

```python
import math

import jax
import jax.numpy as jnp
from jax import lax
from jax.experimental import pallas as pl
from jax.experimental.pallas import tpu as pltpu
from jax.sharding import PartitionSpec as P

QH = 32
KVH = 8
HD = 80
PREFIX = 8192


THETA = 1000000.0
NEG = -1e30


def rotate(values, positions):
    half_dim = values.shape[-1] // 2
    exponent = jnp.arange(half_dim, dtype=jnp.float32) * (2.0 / values.shape[-1])
    inverse = jnp.exp(-exponent * math.log(THETA))
    angles = positions.astype(jnp.float32)[:, None] * inverse[None, :]
    cosine = jnp.cos(angles)[:, None, :]
    sine_part = jnp.sin(angles)[:, None, :]
    first_half = values[..., :half_dim]
    second = values[..., half_dim:]
    return jnp.concatenate(
        [first_half * cosine - second * sine_part, second * cosine + first_half * sine_part],
        axis=-1,
    )


def request_info(request_lens, tok_index):
    request_ends = jnp.cumsum(request_lens)
    passed = tok_index[:, None] >= request_ends[None, :]
    request_of = jnp.sum(passed.astype(jnp.int32), axis=1)
    request_start = jnp.sum(jnp.where(passed, request_lens[None, :], 0), axis=1)
    return (request_of, request_start)


def attn_kernel(sc_ref, q_ref, k_ref, v_ref, st_in, st_ref, *, pre_len):
    rows = q_ref.shape[0]
    suf_len = k_ref.shape[1] - pre_len
    scale = HD ** (-0.5)
    q = q_ref[...]
    kt = k_ref[...]
    vt = v_ref[...]
    st = st_in[...]
    acc = st[:, :HD]
    l = st[:, HD:HD + 1]
    m = st[:, HD + 1:HD + 2]
    s_pre = jnp.dot(q, kt[:, :pre_len], preferred_element_type=jnp.float32) * scale
    s_suf = jnp.dot(q, kt[:, pre_len:], preferred_element_type=jnp.float32) * scale
    qi = sc_ref[1] + lax.broadcasted_iota(jnp.int32, (rows, 1), 0) % suf_len
    qs = jnp.zeros((rows, 1), jnp.int32)
    for j in range(3):
        qs = qs + jnp.where(qi >= sc_ref[2 + 2 * j], sc_ref[3 + 2 * j], 0)
    kidx = sc_ref[0] + lax.broadcasted_iota(jnp.int32, (rows, suf_len), 1)
    mask = (kidx >= qs) & (kidx <= qi)
    s_suf = jnp.where(mask, s_suf, NEG)
    m_new = jnp.maximum(
        m,
        jnp.maximum(jnp.max(s_pre, axis=1, keepdims=True), jnp.max(s_suf, axis=1, keepdims=True)),
    )
    alpha = jnp.exp(m - m_new)
    p_pre = jnp.exp(s_pre - m_new)
    p_suf = jnp.where(mask, jnp.exp(s_suf - m_new), 0.0)
    l_new = alpha * l + (
        jnp.sum(p_pre, axis=1, keepdims=True) + jnp.sum(p_suf, axis=1, keepdims=True)
    )
    nt = (((1,), (1,)), ((), ()))
    pv = lax.dot_general(
        p_pre.astype(jnp.bfloat16), vt[:, :pre_len], nt, preferred_element_type=jnp.float32
    ) + lax.dot_general(
        p_suf.astype(jnp.bfloat16), vt[:, pre_len:], nt, preferred_element_type=jnp.float32
    )
    st_ref[:, :HD] = alpha * acc + pv
    st_ref[:, HD:HD + 1] = l_new
    st_ref[:, HD + 1:HD + 2] = m_new


def attention_block(q_heads, kv_blk, scalars, state, pre_len):
    heads, rows, _ = q_heads.shape
    width = kv_blk.shape[1]
    kernel = lambda *refs: attn_kernel(*refs, pre_len=pre_len)
    st_spec = pl.BlockSpec((None, rows, state.shape[2]), lambda h: (h, 0, 0))
    return pl.pallas_call(
        kernel,
        grid=(heads,),
        in_specs=[
            pl.BlockSpec(memory_space=pltpu.SMEM),
            pl.BlockSpec((None, rows, HD), lambda h: (h, 0, 0)),
            pl.BlockSpec((HD, width), lambda h: (h, 0)),
            pl.BlockSpec((HD, width), lambda h: (heads + h, 0)),
            st_spec,
        ],
        out_specs=st_spec,
        out_shape=jax.ShapeDtypeStruct(state.shape, jnp.float32),
        input_output_aliases={4: 0},
        cost_estimate=pl.CostEstimate(
            flops=4 * heads * rows * width * HD,
            transcendentals=heads * rows * width,
            bytes_accessed=2 * kv_blk.size + 8 * state.size,
        ),
        compiler_params=pltpu.CompilerParams(
            dimension_semantics=("arbitrary",), vmem_limit_bytes=48 * 1024 * 1024
        ),
    )(scalars, q_heads, kv_blk, kv_blk, state)


def body(
    residual,
    queries,
    suffix_kv,
    prefix_kv,
    page_table,
    suffix_lens,
    w_out,
    norm_gain,
    w_gate,
    w_up,
    w_down,
):
    tok_rows = queries.shape[0]
    kv_width = KVH * HD
    per_group = QH // KVH
    tok_index = lax.axis_index("kv") * tok_rows + jnp.arange(tok_rows, dtype=jnp.int32)
    request_lens = suffix_lens[0]
    request_of, request_start = request_info(request_lens, tok_index)
    positions = PREFIX + tok_index - request_start
    rotated_q = rotate(queries.astype(jnp.float32).reshape(tok_rows, QH, HD), positions).astype(
        jnp.bfloat16
    )
    q_heads = (
        rotated_q.reshape(tok_rows, KVH, per_group, HD)
        .transpose(1, 2, 0, 3)
        .reshape(KVH, per_group * tok_rows, HD)
    )
    page_count = prefix_kv.shape[0]
    page_size = prefix_kv.shape[1]
    pre_len = page_count * page_size
    key_count = pre_len + tok_rows
    page_pos = (
        page_table[:, None] * page_size + jnp.arange(page_size, dtype=jnp.int32)[None, :]
    ).reshape(-1)
    key_pos = jnp.concatenate([page_pos, positions]).astype(jnp.float32)
    raw_t = jnp.concatenate(
        [prefix_kv.reshape(pre_len, 2 * kv_width), suffix_kv], axis=0
    ).T
    half_dim = HD // 2
    exponent = jnp.arange(half_dim, dtype=jnp.float32) * (2.0 / HD)
    inverse = jnp.exp(-exponent * math.log(THETA))
    angles = inverse[:, None] * key_pos[None, :]
    cosine = jnp.cos(angles)[None]
    sine_part = jnp.sin(angles)[None]
    halves = raw_t[:kv_width].astype(jnp.float32).reshape(KVH, 2, half_dim, key_count)
    first_half = halves[:, 0]
    second = halves[:, 1]
    keys_t = jnp.stack(
        [first_half * cosine - second * sine_part, second * cosine + first_half * sine_part],
        axis=1,
    ).astype(jnp.bfloat16)
    values_t = raw_t[kv_width:]
    local_t = jnp.concatenate([keys_t.reshape(kv_width, key_count), values_t], axis=0)
    request_ends = jnp.cumsum(request_lens)
    base_scalars = jnp.stack(
        [tok_index[0]]
        + [v for j in range(3) for v in (request_ends[j], request_lens[j])]
    ).astype(jnp.int32)
    rows = per_group * tok_rows
    state = jnp.zeros((KVH, rows, 128), jnp.float32).at[:, :, HD + 1].set(NEG)
    n_kv = lax.axis_size("kv")
    me = lax.axis_index("kv")

    def absorb_block(state, blk, owner):
        scalars = jnp.concatenate([jnp.reshape(owner * tok_rows, (1,)), base_scalars])
        return attention_block(q_heads, blk, scalars.astype(jnp.int32), state, pre_len)

    cw_pairs = [(i, (i + 1) % n_kv) for i in range(n_kv)]
    ccw_pairs = [(i, (i - 1) % n_kv) for i in range(n_kv)]
    prev_state = state
    state = absorb_block(state, local_t, me)
    cw_blk = local_t
    ccw_blk = local_t
    for step in range(1, n_kv // 2 + 1):
        if step > 1:
            (cw_blk, ccw_blk), unused = lax.optimization_barrier(((cw_blk, ccw_blk), prev_state))
        prev_state = state
        cw_blk = lax.ppermute(cw_blk, "kv", cw_pairs)
        if step < n_kv - step:
            ccw_blk = lax.ppermute(ccw_blk, "kv", ccw_pairs)
        state = absorb_block(state, cw_blk, (me - step) % n_kv)
        if step < n_kv - step:
            state = absorb_block(state, ccw_blk, (me + step) % n_kv)
    out_heads = (state[:, :, :HD] / state[:, :, HD:HD + 1]).astype(jnp.bfloat16)
    attended = (
        out_heads.reshape(KVH, per_group, tok_rows, HD)
        .transpose(2, 0, 1, 3)
        .reshape(tok_rows, QH * HD)
    )
    mixed_sum = residual.astype(jnp.float32) + jnp.dot(
        attended, w_out, preferred_element_type=jnp.float32
    )
    stream_wide = mixed_sum.astype(jnp.bfloat16).astype(jnp.float32)
    normed = (
        stream_wide
        * lax.rsqrt(jnp.mean(stream_wide * stream_wide, axis=1, keepdims=True) + 1e-05)
        * norm_gain
    ).astype(jnp.bfloat16)
    shard_piece = lax.all_gather(normed, "req", axis=0, tiled=True)
    gate_proj = jnp.dot(shard_piece, w_gate, preferred_element_type=jnp.float32)
    up_proj = jnp.dot(shard_piece, w_up, preferred_element_type=jnp.float32)
    activated = (jax.nn.silu(gate_proj) * up_proj).astype(jnp.bfloat16)
    summed = lax.psum_scatter(
        jnp.dot(activated, w_down, preferred_element_type=jnp.float32).astype(jnp.bfloat16),
        "req",
        scatter_dimension=0,
        tiled=True,
    ).astype(jnp.float32)
    layer_out = (stream_wide + summed).astype(jnp.bfloat16)
    return (attended, layer_out)


def solution(mesh):
    in_specs = (
        P(("req", "kv"), None),
        P(("req", "kv"), None),
        P(("req", "kv"), None),
        P("kv", None, None),
        P("kv"),
        P("req", None),
        P(),
        P(),
        P(None, "req"),
        P(None, "req"),
        P("req", None),
    )
    out_specs = (P(("req", "kv"), None), P(("req", "kv"), None))
    return jax.shard_map(body, mesh=mesh, in_specs=in_specs, out_specs=out_specs, check_vma=False)
```

```python
import math

import jax
import jax.numpy as jnp
from jax import lax
from jax.experimental import pallas as pl
from jax.experimental.pallas import tpu as pltpu
from jax.sharding import PartitionSpec as P

QH = 32
KVH = 8
HD = 80
PREFIX = 8192


THETA = 1000000.0
NEG = -1e30


def rotate(values, positions):
    half_dim = values.shape[-1] // 2
    exponent = jnp.arange(half_dim, dtype=jnp.float32) * (2.0 / values.shape[-1])
    inverse = jnp.exp(-exponent * math.log(THETA))
    angles = positions.astype(jnp.float32)[:, None] * inverse[None, :]
    cosine = jnp.cos(angles)[:, None, :]
    sine_part = jnp.sin(angles)[:, None, :]
    first_half = values[..., :half_dim]
    second = values[..., half_dim:]
    return jnp.concatenate(
        [first_half * cosine - second * sine_part, second * cosine + first_half * sine_part],
        axis=-1,
    )


def request_info(request_lens, tok_index):
    request_ends = jnp.cumsum(request_lens)
    passed = tok_index[:, None] >= request_ends[None, :]
    request_of = jnp.sum(passed.astype(jnp.int32), axis=1)
    request_start = jnp.sum(jnp.where(passed, request_lens[None, :], 0), axis=1)
    return (request_of, request_start)


def attn_kernel(off_ref, sc_ref, q_ref, k_ref, v_ref, st_in, st_ref, *, pre_len):
    rows = q_ref.shape[0]
    suf_len = k_ref.shape[1] - pre_len
    scale = HD ** (-0.5)
    q = q_ref[...]
    kt = k_ref[...]
    vt = v_ref[...]
    st = st_in[...]
    acc = st[:, :HD]
    l = st[:, HD:HD + 1]
    m = st[:, HD + 1:HD + 2]
    s_pre = jnp.dot(q, kt[:, :pre_len], preferred_element_type=jnp.float32) * scale
    s_suf = jnp.dot(q, kt[:, pre_len:], preferred_element_type=jnp.float32) * scale
    qi = sc_ref[0] + lax.broadcasted_iota(jnp.int32, (rows, 1), 0) % suf_len
    qs = jnp.zeros((rows, 1), jnp.int32)
    for j in range(3):
        qs = qs + jnp.where(qi >= sc_ref[1 + 2 * j], sc_ref[2 + 2 * j], 0)
    kidx = off_ref[0] + lax.broadcasted_iota(jnp.int32, (rows, suf_len), 1)
    mask = (kidx >= qs) & (kidx <= qi)
    s_suf = jnp.where(mask, s_suf, NEG)
    m_new = jnp.maximum(
        m,
        jnp.maximum(jnp.max(s_pre, axis=1, keepdims=True), jnp.max(s_suf, axis=1, keepdims=True)),
    )
    alpha = jnp.exp(m - m_new)
    p_pre = jnp.exp(s_pre - m_new)
    p_suf = jnp.where(mask, jnp.exp(s_suf - m_new), 0.0)
    l_new = alpha * l + (
        jnp.sum(p_pre, axis=1, keepdims=True) + jnp.sum(p_suf, axis=1, keepdims=True)
    )
    nt = (((1,), (1,)), ((), ()))
    pv = lax.dot_general(
        p_pre.astype(jnp.bfloat16), vt[:, :pre_len], nt, preferred_element_type=jnp.float32
    ) + lax.dot_general(
        p_suf.astype(jnp.bfloat16), vt[:, pre_len:], nt, preferred_element_type=jnp.float32
    )
    st_ref[:, :HD] = alpha * acc + pv
    st_ref[:, HD:HD + 1] = l_new
    st_ref[:, HD + 1:HD + 2] = m_new


def attention_block(q_heads, kv_blk, offset, scalars, state, pre_len):
    heads, rows, _ = q_heads.shape
    width = kv_blk.shape[1]
    kernel = lambda *refs: attn_kernel(*refs, pre_len=pre_len)
    st_spec = pl.BlockSpec((None, rows, state.shape[2]), lambda h: (h, 0, 0))
    return pl.pallas_call(
        kernel,
        grid=(heads,),
        in_specs=[
            pl.BlockSpec(memory_space=pltpu.SMEM),
            pl.BlockSpec(memory_space=pltpu.SMEM),
            pl.BlockSpec((None, rows, HD), lambda h: (h, 0, 0)),
            pl.BlockSpec((HD, width), lambda h: (h, 0)),
            pl.BlockSpec((HD, width), lambda h: (heads + h, 0)),
            st_spec,
        ],
        out_specs=st_spec,
        out_shape=jax.ShapeDtypeStruct(state.shape, jnp.float32),
        input_output_aliases={5: 0},
        cost_estimate=pl.CostEstimate(
            flops=4 * heads * rows * width * HD,
            transcendentals=heads * rows * width,
            bytes_accessed=2 * kv_blk.size + 8 * state.size,
        ),
        compiler_params=pltpu.CompilerParams(
            dimension_semantics=("arbitrary",), vmem_limit_bytes=48 * 1024 * 1024
        ),
    )(offset, scalars, q_heads, kv_blk, kv_blk, state)


def body(
    residual,
    queries,
    suffix_kv,
    prefix_kv,
    page_table,
    suffix_lens,
    w_out,
    norm_gain,
    w_gate,
    w_up,
    w_down,
):
    tok_rows = queries.shape[0]
    kv_width = KVH * HD
    per_group = QH // KVH
    tok_index = lax.axis_index("kv") * tok_rows + jnp.arange(tok_rows, dtype=jnp.int32)
    request_lens = suffix_lens[0]
    request_of, request_start = request_info(request_lens, tok_index)
    positions = PREFIX + tok_index - request_start
    rotated_q = rotate(queries.astype(jnp.float32).reshape(tok_rows, QH, HD), positions).astype(
        jnp.bfloat16
    )
    q_heads = (
        rotated_q.reshape(tok_rows, KVH, per_group, HD)
        .transpose(1, 2, 0, 3)
        .reshape(KVH, per_group * tok_rows, HD)
    )
    page_count = prefix_kv.shape[0]
    page_size = prefix_kv.shape[1]
    pre_len = page_count * page_size
    key_count = pre_len + tok_rows
    page_pos = (
        page_table[:, None] * page_size + jnp.arange(page_size, dtype=jnp.int32)[None, :]
    ).reshape(-1)
    key_pos = jnp.concatenate([page_pos, positions]).astype(jnp.float32)
    raw_t = jnp.concatenate(
        [prefix_kv.reshape(pre_len, 2 * kv_width), suffix_kv], axis=0
    ).T
    half_dim = HD // 2
    exponent = jnp.arange(half_dim, dtype=jnp.float32) * (2.0 / HD)
    inverse = jnp.exp(-exponent * math.log(THETA))
    angles = inverse[:, None] * key_pos[None, :]
    cosine = jnp.cos(angles)[None]
    sine_part = jnp.sin(angles)[None]
    halves = raw_t[:kv_width].astype(jnp.float32).reshape(KVH, 2, half_dim, key_count)
    first_half = halves[:, 0]
    second = halves[:, 1]
    keys_t = jnp.stack(
        [first_half * cosine - second * sine_part, second * cosine + first_half * sine_part],
        axis=1,
    ).astype(jnp.bfloat16)
    values_t = raw_t[kv_width:]
    local_t = jnp.concatenate([keys_t.reshape(kv_width, key_count), values_t], axis=0)
    request_ends = jnp.cumsum(request_lens)
    base_scalars = jnp.stack(
        [tok_index[0]]
        + [v for j in range(3) for v in (request_ends[j], request_lens[j])]
    ).astype(jnp.int32)
    rows = per_group * tok_rows
    state = jnp.zeros((KVH, rows, 128), jnp.float32).at[:, :, HD + 1].set(NEG)
    n_kv = lax.axis_size("kv")
    me = lax.axis_index("kv")

    def absorb_block(state, blk, owner):
        offset = jnp.reshape(owner * tok_rows, (1,)).astype(jnp.int32)
        return attention_block(q_heads, blk, offset, base_scalars, state, pre_len)

    cw_pairs = [(i, (i + 1) % n_kv) for i in range(n_kv)]
    ccw_pairs = [(i, (i - 1) % n_kv) for i in range(n_kv)]
    prev_state = state
    state = absorb_block(state, local_t, me)
    cw_blk = local_t
    ccw_blk = local_t
    for step in range(1, n_kv // 2 + 1):
        if step > 1:
            (cw_blk, ccw_blk), unused = lax.optimization_barrier(((cw_blk, ccw_blk), prev_state))
        prev_state = state
        cw_blk = lax.ppermute(cw_blk, "kv", cw_pairs)
        if step < n_kv - step:
            ccw_blk = lax.ppermute(ccw_blk, "kv", ccw_pairs)
        state = absorb_block(state, cw_blk, (me - step) % n_kv)
        if step < n_kv - step:
            state = absorb_block(state, ccw_blk, (me + step) % n_kv)
    out_heads = (state[:, :, :HD] / state[:, :, HD:HD + 1]).astype(jnp.bfloat16)
    attended = (
        out_heads.reshape(KVH, per_group, tok_rows, HD)
        .transpose(2, 0, 1, 3)
        .reshape(tok_rows, QH * HD)
    )
    mixed_sum = residual.astype(jnp.float32) + jnp.dot(
        attended, w_out, preferred_element_type=jnp.float32
    )
    stream_wide = mixed_sum.astype(jnp.bfloat16).astype(jnp.float32)
    normed = (
        stream_wide
        * lax.rsqrt(jnp.mean(stream_wide * stream_wide, axis=1, keepdims=True) + 1e-05)
        * norm_gain
    ).astype(jnp.bfloat16)
    shard_piece = lax.all_gather(normed, "req", axis=0, tiled=True)
    gate_proj = jnp.dot(shard_piece, w_gate, preferred_element_type=jnp.float32)
    up_proj = jnp.dot(shard_piece, w_up, preferred_element_type=jnp.float32)
    activated = (jax.nn.silu(gate_proj) * up_proj).astype(jnp.bfloat16)
    summed = lax.psum_scatter(
        jnp.dot(activated, w_down, preferred_element_type=jnp.float32).astype(jnp.bfloat16),
        "req",
        scatter_dimension=0,
        tiled=True,
    ).astype(jnp.float32)
    layer_out = (stream_wide + summed).astype(jnp.bfloat16)
    return (attended, layer_out)


def solution(mesh):
    in_specs = (
        P(("req", "kv"), None),
        P(("req", "kv"), None),
        P(("req", "kv"), None),
        P("kv", None, None),
        P("kv"),
        P("req", None),
        P(),
        P(),
        P(None, "req"),
        P(None, "req"),
        P("req", None),
    )
    out_specs = (P(("req", "kv"), None), P(("req", "kv"), None))
    return jax.shard_map(body, mesh=mesh, in_specs=in_specs, out_specs=out_specs, check_vma=False)
```

```python
import math

import jax
import jax.numpy as jnp
from jax import lax
from jax.experimental import pallas as pl
from jax.experimental.pallas import tpu as pltpu
from jax.sharding import PartitionSpec as P

QH = 32
KVH = 8
HD = 80
PREFIX = 8192


THETA = 1000000.0
NEG = -1e30


def rotate(values, positions):
    half_dim = values.shape[-1] // 2
    exponent = jnp.arange(half_dim, dtype=jnp.float32) * (2.0 / values.shape[-1])
    inverse = jnp.exp(-exponent * math.log(THETA))
    angles = positions.astype(jnp.float32)[:, None] * inverse[None, :]
    cosine = jnp.cos(angles)[:, None, :]
    sine_part = jnp.sin(angles)[:, None, :]
    first_half = values[..., :half_dim]
    second = values[..., half_dim:]
    return jnp.concatenate(
        [first_half * cosine - second * sine_part, second * cosine + first_half * sine_part],
        axis=-1,
    )


def request_info(request_lens, tok_index):
    request_ends = jnp.cumsum(request_lens)
    passed = tok_index[:, None] >= request_ends[None, :]
    request_of = jnp.sum(passed.astype(jnp.int32), axis=1)
    request_start = jnp.sum(jnp.where(passed, request_lens[None, :], 0), axis=1)
    return (request_of, request_start)


def attn_kernel(off_ref, sc_ref, q_ref, k_ref, v_ref, st_in, st_ref, *, pre_len):
    rows = q_ref.shape[0]
    suf_len = k_ref.shape[1] - pre_len
    scale = HD ** (-0.5)
    q = q_ref[...]
    kt = k_ref[...]
    vt = v_ref[...]
    st = st_in[...]
    acc = st[:, :HD]
    l = st[:, HD:HD + 1]
    m = st[:, HD + 1:HD + 2]
    s_pre = jnp.dot(q, kt[:, :pre_len], preferred_element_type=jnp.float32) * scale
    s_suf = jnp.dot(q, kt[:, pre_len:], preferred_element_type=jnp.float32) * scale
    qi = sc_ref[0] + lax.broadcasted_iota(jnp.int32, (rows, 1), 0) % suf_len
    qs = jnp.zeros((rows, 1), jnp.int32)
    for j in range(3):
        qs = qs + jnp.where(qi >= sc_ref[1 + 2 * j], sc_ref[2 + 2 * j], 0)
    kidx = off_ref[0] + lax.broadcasted_iota(jnp.int32, (rows, suf_len), 1)
    mask = (kidx >= qs) & (kidx <= qi)
    s_suf = jnp.where(mask, s_suf, NEG)
    m_new = jnp.maximum(
        m,
        jnp.maximum(jnp.max(s_pre, axis=1, keepdims=True), jnp.max(s_suf, axis=1, keepdims=True)),
    )
    alpha = jnp.exp(m - m_new)
    p_pre = jnp.exp(s_pre - m_new)
    p_suf = jnp.where(mask, jnp.exp(s_suf - m_new), 0.0)
    l_new = alpha * l + (
        jnp.sum(p_pre, axis=1, keepdims=True) + jnp.sum(p_suf, axis=1, keepdims=True)
    )
    nt = (((1,), (1,)), ((), ()))
    pv = lax.dot_general(
        p_pre.astype(jnp.bfloat16), vt[:, :pre_len], nt, preferred_element_type=jnp.float32
    ) + lax.dot_general(
        p_suf.astype(jnp.bfloat16), vt[:, pre_len:], nt, preferred_element_type=jnp.float32
    )
    st_ref[:, :HD] = alpha * acc + pv
    st_ref[:, HD:HD + 1] = l_new
    st_ref[:, HD + 1:HD + 2] = m_new


def attention_block(q_heads, kv_blk, offset, scalars, state, pre_len):
    heads, rows, _ = q_heads.shape
    width = kv_blk.shape[1]
    kernel = lambda *refs: attn_kernel(*refs, pre_len=pre_len)
    st_spec = pl.BlockSpec((None, rows, state.shape[2]), lambda h: (h, 0, 0))
    return pl.pallas_call(
        kernel,
        grid=(heads,),
        in_specs=[
            pl.BlockSpec(memory_space=pltpu.SMEM),
            pl.BlockSpec(memory_space=pltpu.SMEM),
            pl.BlockSpec((None, rows, HD), lambda h: (h, 0, 0)),
            pl.BlockSpec((HD, width), lambda h: (h, 0)),
            pl.BlockSpec((HD, width), lambda h: (heads + h, 0)),
            st_spec,
        ],
        out_specs=st_spec,
        out_shape=jax.ShapeDtypeStruct(state.shape, jnp.float32),
        input_output_aliases={5: 0},
        cost_estimate=pl.CostEstimate(
            flops=4 * heads * rows * width * HD,
            transcendentals=heads * rows * width,
            bytes_accessed=2 * kv_blk.size + 8 * state.size,
        ),
        compiler_params=pltpu.CompilerParams(
            dimension_semantics=("arbitrary",), vmem_limit_bytes=48 * 1024 * 1024
        ),
    )(offset, scalars, q_heads, kv_blk, kv_blk, state)


def body(
    residual,
    queries,
    suffix_kv,
    prefix_kv,
    page_table,
    suffix_lens,
    w_out,
    norm_gain,
    w_gate,
    w_up,
    w_down,
):
    tok_rows = queries.shape[0]
    kv_width = KVH * HD
    per_group = QH // KVH
    tok_index = lax.axis_index("kv") * tok_rows + jnp.arange(tok_rows, dtype=jnp.int32)
    request_lens = suffix_lens[0]
    request_of, request_start = request_info(request_lens, tok_index)
    positions = PREFIX + tok_index - request_start
    rotated_q = rotate(queries.astype(jnp.float32).reshape(tok_rows, QH, HD), positions).astype(
        jnp.bfloat16
    )
    q_heads = (
        rotated_q.reshape(tok_rows, KVH, per_group, HD)
        .transpose(1, 2, 0, 3)
        .reshape(KVH, per_group * tok_rows, HD)
    )
    page_count = prefix_kv.shape[0]
    page_size = prefix_kv.shape[1]
    pre_len = page_count * page_size
    key_count = pre_len + tok_rows
    page_pos = (
        page_table[:, None] * page_size + jnp.arange(page_size, dtype=jnp.int32)[None, :]
    ).reshape(-1)
    key_pos = jnp.concatenate([page_pos, positions]).astype(jnp.float32)
    raw_t = jnp.concatenate(
        [prefix_kv.reshape(pre_len, 2 * kv_width), suffix_kv], axis=0
    ).T
    half_dim = HD // 2
    exponent = jnp.arange(half_dim, dtype=jnp.float32) * (2.0 / HD)
    inverse = jnp.exp(-exponent * math.log(THETA))
    angles = inverse[:, None] * key_pos[None, :]
    cosine = jnp.cos(angles)[None]
    sine_part = jnp.sin(angles)[None]
    halves = raw_t[:kv_width].astype(jnp.float32).reshape(KVH, 2, half_dim, key_count)
    first_half = halves[:, 0]
    second = halves[:, 1]
    keys_t = jnp.stack(
        [first_half * cosine - second * sine_part, second * cosine + first_half * sine_part],
        axis=1,
    ).astype(jnp.bfloat16)
    values_t = raw_t[kv_width:]
    local_t = jnp.concatenate([keys_t.reshape(kv_width, key_count), values_t], axis=0)
    request_ends = jnp.cumsum(request_lens)
    base_scalars = jnp.stack(
        [tok_index[0]]
        + [v for j in range(3) for v in (request_ends[j], request_lens[j])]
    ).astype(jnp.int32)
    rows = per_group * tok_rows
    state = jnp.zeros((KVH, rows, 128), jnp.float32).at[:, :, HD + 1].set(NEG)
    n_kv = lax.axis_size("kv")
    me = lax.axis_index("kv")

    def absorb_block(state, blk, owner):
        offset = jnp.reshape(owner * tok_rows, (1,)).astype(jnp.int32)
        return attention_block(q_heads, blk, offset, base_scalars, state, pre_len)

    cw_pairs = [(i, (i + 1) % n_kv) for i in range(n_kv)]
    ccw_pairs = [(i, (i - 1) % n_kv) for i in range(n_kv)]
    prev_state = state
    state = absorb_block(state, local_t, me)
    cw_blk = local_t
    ccw_blk = local_t
    for step in range(1, n_kv // 2 + 1):
        if step > 1:
            (cw_blk, ccw_blk), unused = lax.optimization_barrier(((cw_blk, ccw_blk), prev_state))
        prev_state = state
        if step == n_kv - step:
            split = 4 * 128
            cw_part = lax.ppermute(cw_blk[:, :split], "kv", cw_pairs)
            ccw_part = lax.ppermute(ccw_blk[:, split:], "kv", ccw_pairs)
            cw_blk = jnp.concatenate([cw_part, ccw_part], axis=1)
        else:
            cw_blk = lax.ppermute(cw_blk, "kv", cw_pairs)
        if step < n_kv - step:
            ccw_blk = lax.ppermute(ccw_blk, "kv", ccw_pairs)
        state = absorb_block(state, cw_blk, (me - step) % n_kv)
        if step < n_kv - step:
            state = absorb_block(state, ccw_blk, (me + step) % n_kv)
    out_heads = (state[:, :, :HD] / state[:, :, HD:HD + 1]).astype(jnp.bfloat16)
    attended = (
        out_heads.reshape(KVH, per_group, tok_rows, HD)
        .transpose(2, 0, 1, 3)
        .reshape(tok_rows, QH * HD)
    )
    mixed_sum = residual.astype(jnp.float32) + jnp.dot(
        attended, w_out, preferred_element_type=jnp.float32
    )
    stream_wide = mixed_sum.astype(jnp.bfloat16).astype(jnp.float32)
    normed = (
        stream_wide
        * lax.rsqrt(jnp.mean(stream_wide * stream_wide, axis=1, keepdims=True) + 1e-05)
        * norm_gain
    ).astype(jnp.bfloat16)
    shard_piece = lax.all_gather(normed, "req", axis=0, tiled=True)
    gate_proj = jnp.dot(shard_piece, w_gate, preferred_element_type=jnp.float32)
    up_proj = jnp.dot(shard_piece, w_up, preferred_element_type=jnp.float32)
    activated = (jax.nn.silu(gate_proj) * up_proj).astype(jnp.bfloat16)
    summed = lax.psum_scatter(
        jnp.dot(activated, w_down, preferred_element_type=jnp.float32).astype(jnp.bfloat16),
        "req",
        scatter_dimension=0,
        tiled=True,
    ).astype(jnp.float32)
    layer_out = (stream_wide + summed).astype(jnp.bfloat16)
    return (attended, layer_out)


def solution(mesh):
    in_specs = (
        P(("req", "kv"), None),
        P(("req", "kv"), None),
        P(("req", "kv"), None),
        P("kv", None, None),
        P("kv"),
        P("req", None),
        P(),
        P(),
        P(None, "req"),
        P(None, "req"),
        P("req", None),
    )
    out_specs = (P(("req", "kv"), None), P(("req", "kv"), None))
    return jax.shard_map(body, mesh=mesh, in_specs=in_specs, out_specs=out_specs, check_vma=False)
```

```python
import math

import jax
import jax.numpy as jnp
from jax import lax
from jax.experimental import pallas as pl
from jax.experimental.pallas import tpu as pltpu
from jax.sharding import PartitionSpec as P

QH = 32
KVH = 8
HD = 80
PREFIX = 8192


THETA = 1000000.0
NEG = -1e30


def rotate(values, positions):
    half_dim = values.shape[-1] // 2
    exponent = jnp.arange(half_dim, dtype=jnp.float32) * (2.0 / values.shape[-1])
    inverse = jnp.exp(-exponent * math.log(THETA))
    angles = positions.astype(jnp.float32)[:, None] * inverse[None, :]
    cosine = jnp.cos(angles)[:, None, :]
    sine_part = jnp.sin(angles)[:, None, :]
    first_half = values[..., :half_dim]
    second = values[..., half_dim:]
    return jnp.concatenate(
        [first_half * cosine - second * sine_part, second * cosine + first_half * sine_part],
        axis=-1,
    )


def request_info(request_lens, tok_index):
    request_ends = jnp.cumsum(request_lens)
    passed = tok_index[:, None] >= request_ends[None, :]
    request_of = jnp.sum(passed.astype(jnp.int32), axis=1)
    request_start = jnp.sum(jnp.where(passed, request_lens[None, :], 0), axis=1)
    return (request_of, request_start)


def attn_kernel(off_ref, sc_ref, q_ref, k_ref, v_ref, st_in, st_ref, *, pre_len):
    rows = q_ref.shape[0]
    suf_len = k_ref.shape[1] - pre_len
    scale = HD ** (-0.5)
    q = q_ref[...]
    kt = k_ref[...]
    vt = v_ref[...]
    st = st_in[...]
    acc = st[:, :HD]
    l = st[:, HD:HD + 1]
    m = st[:, HD + 1:HD + 2]
    s_pre = jnp.dot(q, kt[:, :pre_len], preferred_element_type=jnp.float32) * scale
    s_suf = jnp.dot(q, kt[:, pre_len:], preferred_element_type=jnp.float32) * scale
    qi = sc_ref[0] + lax.broadcasted_iota(jnp.int32, (rows, 1), 0) % suf_len
    qs = jnp.zeros((rows, 1), jnp.int32)
    for j in range(3):
        qs = qs + jnp.where(qi >= sc_ref[1 + 2 * j], sc_ref[2 + 2 * j], 0)
    kidx = off_ref[0] + lax.broadcasted_iota(jnp.int32, (rows, suf_len), 1)
    mask = (kidx >= qs) & (kidx <= qi)
    s_suf = jnp.where(mask, s_suf, NEG)
    m_new = jnp.maximum(
        m,
        jnp.maximum(jnp.max(s_pre, axis=1, keepdims=True), jnp.max(s_suf, axis=1, keepdims=True)),
    )
    alpha = jnp.exp(m - m_new)
    p_pre = jnp.exp(s_pre - m_new)
    p_suf = jnp.where(mask, jnp.exp(s_suf - m_new), 0.0)
    l_new = alpha * l + (
        jnp.sum(p_pre, axis=1, keepdims=True) + jnp.sum(p_suf, axis=1, keepdims=True)
    )
    nt = (((1,), (1,)), ((), ()))
    pv = lax.dot_general(
        p_pre.astype(jnp.bfloat16), vt[:, :pre_len], nt, preferred_element_type=jnp.float32
    ) + lax.dot_general(
        p_suf.astype(jnp.bfloat16), vt[:, pre_len:], nt, preferred_element_type=jnp.float32
    )
    st_ref[:, :HD] = alpha * acc + pv
    st_ref[:, HD:HD + 1] = l_new
    st_ref[:, HD + 1:HD + 2] = m_new


def attention_block(q_heads, kv_blk, offset, scalars, state, pre_len):
    heads, rows, _ = q_heads.shape
    width = kv_blk.shape[1]
    kernel = lambda *refs: attn_kernel(*refs, pre_len=pre_len)
    st_spec = pl.BlockSpec((None, rows, state.shape[2]), lambda h: (h, 0, 0))
    return pl.pallas_call(
        kernel,
        grid=(heads,),
        in_specs=[
            pl.BlockSpec(memory_space=pltpu.SMEM),
            pl.BlockSpec(memory_space=pltpu.SMEM),
            pl.BlockSpec((None, rows, HD), lambda h: (h, 0, 0)),
            pl.BlockSpec((HD, width), lambda h: (h, 0)),
            pl.BlockSpec((HD, width), lambda h: (heads + h, 0)),
            st_spec,
        ],
        out_specs=st_spec,
        out_shape=jax.ShapeDtypeStruct(state.shape, jnp.float32),
        input_output_aliases={5: 0},
        cost_estimate=pl.CostEstimate(
            flops=4 * heads * rows * width * HD,
            transcendentals=heads * rows * width,
            bytes_accessed=2 * kv_blk.size + 8 * state.size,
        ),
        compiler_params=pltpu.CompilerParams(
            dimension_semantics=("arbitrary",), vmem_limit_bytes=48 * 1024 * 1024
        ),
    )(offset, scalars, q_heads, kv_blk, kv_blk, state)


def body(
    residual,
    queries,
    suffix_kv,
    prefix_kv,
    page_table,
    suffix_lens,
    w_out,
    norm_gain,
    w_gate,
    w_up,
    w_down,
):
    tok_rows = queries.shape[0]
    kv_width = KVH * HD
    per_group = QH // KVH
    tok_index = lax.axis_index("kv") * tok_rows + jnp.arange(tok_rows, dtype=jnp.int32)
    request_lens = suffix_lens[0]
    request_of, request_start = request_info(request_lens, tok_index)
    positions = PREFIX + tok_index - request_start
    rotated_q = rotate(queries.astype(jnp.float32).reshape(tok_rows, QH, HD), positions).astype(
        jnp.bfloat16
    )
    q_heads = (
        rotated_q.reshape(tok_rows, KVH, per_group, HD)
        .transpose(1, 2, 0, 3)
        .reshape(KVH, per_group * tok_rows, HD)
    )
    page_count = prefix_kv.shape[0]
    page_size = prefix_kv.shape[1]
    pre_len = page_count * page_size
    key_count = pre_len + tok_rows
    page_pos = (
        page_table[:, None] * page_size + jnp.arange(page_size, dtype=jnp.int32)[None, :]
    ).reshape(-1)
    key_pos = jnp.concatenate([page_pos, positions]).astype(jnp.float32)
    raw_t = jnp.concatenate(
        [prefix_kv.reshape(pre_len, 2 * kv_width), suffix_kv], axis=0
    ).T
    half_dim = HD // 2
    exponent = jnp.arange(half_dim, dtype=jnp.float32) * (2.0 / HD)
    inverse = jnp.exp(-exponent * math.log(THETA))
    angles = inverse[:, None] * key_pos[None, :]
    cosine = jnp.cos(angles)[None]
    sine_part = jnp.sin(angles)[None]
    halves = raw_t[:kv_width].astype(jnp.float32).reshape(KVH, 2, half_dim, key_count)
    first_half = halves[:, 0]
    second = halves[:, 1]
    keys_t = jnp.stack(
        [first_half * cosine - second * sine_part, second * cosine + first_half * sine_part],
        axis=1,
    ).astype(jnp.bfloat16)
    values_t = raw_t[kv_width:]
    local_t = jnp.concatenate([keys_t.reshape(kv_width, key_count), values_t], axis=0)
    request_ends = jnp.cumsum(request_lens)
    base_scalars = jnp.stack(
        [tok_index[0]]
        + [v for j in range(3) for v in (request_ends[j], request_lens[j])]
    ).astype(jnp.int32)
    rows = per_group * tok_rows
    state = jnp.zeros((KVH, rows, 128), jnp.float32).at[:, :, HD + 1].set(NEG)
    n_kv = lax.axis_size("kv")
    me = lax.axis_index("kv")

    def absorb_block(state, blk, owner):
        offset = jnp.reshape(owner * tok_rows, (1,)).astype(jnp.int32)
        return attention_block(q_heads, blk, offset, base_scalars, state, pre_len)

    cw_pairs = [(i, (i + 1) % n_kv) for i in range(n_kv)]
    ccw_pairs = [(i, (i - 1) % n_kv) for i in range(n_kv)]
    prev_state = state
    state = absorb_block(state, local_t, me)
    cw_blk = local_t
    ccw_blk = local_t
    for step in range(1, n_kv // 2 + 1):
        if step > 1:
            (cw_blk, ccw_blk), unused = lax.optimization_barrier(((cw_blk, ccw_blk), prev_state))
        prev_state = state
        cw_blk = lax.ppermute(cw_blk, "kv", cw_pairs)
        if step < n_kv - step:
            ccw_blk = lax.ppermute(ccw_blk, "kv", ccw_pairs)
        state = absorb_block(state, cw_blk, (me - step) % n_kv)
        if step < n_kv - step:
            state = absorb_block(state, ccw_blk, (me + step) % n_kv)
    out_heads = (state[:, :, :HD] / state[:, :, HD:HD + 1]).astype(jnp.bfloat16)
    attended = (
        out_heads.reshape(KVH, per_group, tok_rows, HD)
        .transpose(2, 0, 1, 3)
        .reshape(tok_rows, QH * HD)
    )
    mixed_sum = residual.astype(jnp.float32) + jnp.dot(
        attended, w_out, preferred_element_type=jnp.float32
    )
    stream_wide = mixed_sum.astype(jnp.bfloat16).astype(jnp.float32)
    normed = (
        stream_wide
        * lax.rsqrt(jnp.mean(stream_wide * stream_wide, axis=1, keepdims=True) + 1e-05)
        * norm_gain
    ).astype(jnp.bfloat16)
    shard_piece = lax.all_gather(normed, "req", axis=0, tiled=True)
    gate_proj = jnp.dot(shard_piece, w_gate, preferred_element_type=jnp.float32)
    up_proj = jnp.dot(shard_piece, w_up, preferred_element_type=jnp.float32)
    activated = (jax.nn.silu(gate_proj) * up_proj).astype(jnp.bfloat16)
    activated = lax.optimization_barrier(activated)
    summed = lax.psum_scatter(
        jnp.dot(activated, w_down, preferred_element_type=jnp.float32).astype(jnp.bfloat16),
        "req",
        scatter_dimension=0,
        tiled=True,
    ).astype(jnp.float32)
    layer_out = (stream_wide + summed).astype(jnp.bfloat16)
    return (attended, layer_out)


def solution(mesh):
    in_specs = (
        P(("req", "kv"), None),
        P(("req", "kv"), None),
        P(("req", "kv"), None),
        P("kv", None, None),
        P("kv"),
        P("req", None),
        P(),
        P(),
        P(None, "req"),
        P(None, "req"),
        P("req", None),
    )
    out_specs = (P(("req", "kv"), None), P(("req", "kv"), None))
    return jax.shard_map(body, mesh=mesh, in_specs=in_specs, out_specs=out_specs, check_vma=False)
```

```python
import math

import jax
import jax.numpy as jnp
from jax import lax
from jax.experimental import pallas as pl
from jax.experimental.pallas import tpu as pltpu
from jax.sharding import PartitionSpec as P

QH = 32
KVH = 8
HD = 80
PREFIX = 8192


THETA = 1000000.0
NEG = -1e30


def rotate(values, positions):
    half_dim = values.shape[-1] // 2
    exponent = jnp.arange(half_dim, dtype=jnp.float32) * (2.0 / values.shape[-1])
    inverse = jnp.exp(-exponent * math.log(THETA))
    angles = positions.astype(jnp.float32)[:, None] * inverse[None, :]
    cosine = jnp.cos(angles)[:, None, :]
    sine_part = jnp.sin(angles)[:, None, :]
    first_half = values[..., :half_dim]
    second = values[..., half_dim:]
    return jnp.concatenate(
        [first_half * cosine - second * sine_part, second * cosine + first_half * sine_part],
        axis=-1,
    )


def request_info(request_lens, tok_index):
    request_ends = jnp.cumsum(request_lens)
    passed = tok_index[:, None] >= request_ends[None, :]
    request_of = jnp.sum(passed.astype(jnp.int32), axis=1)
    request_start = jnp.sum(jnp.where(passed, request_lens[None, :], 0), axis=1)
    return (request_of, request_start)


def attn_kernel(off_ref, sc_ref, q_ref, k_ref, v_ref, st_in, st_ref, *, pre_len):
    rows = q_ref.shape[0]
    suf_len = k_ref.shape[1] - pre_len
    scale = HD ** (-0.5)
    q = q_ref[...]
    kt = k_ref[...]
    vt = v_ref[...]
    st = st_in[...]
    acc = st[:, :HD]
    l = st[:, HD:HD + 1]
    m = st[:, HD + 1:HD + 2]
    s_pre = jnp.dot(q, kt[:, :pre_len], preferred_element_type=jnp.float32) * scale
    s_suf = jnp.dot(q, kt[:, pre_len:], preferred_element_type=jnp.float32) * scale
    qi = sc_ref[0] + lax.broadcasted_iota(jnp.int32, (rows, 1), 0) % suf_len
    qs = jnp.zeros((rows, 1), jnp.int32)
    for j in range(3):
        qs = qs + jnp.where(qi >= sc_ref[1 + 2 * j], sc_ref[2 + 2 * j], 0)
    kidx = off_ref[0] + lax.broadcasted_iota(jnp.int32, (rows, suf_len), 1)
    mask = (kidx >= qs) & (kidx <= qi)
    s_suf = jnp.where(mask, s_suf, NEG)
    m_new = jnp.maximum(
        m,
        jnp.maximum(jnp.max(s_pre, axis=1, keepdims=True), jnp.max(s_suf, axis=1, keepdims=True)),
    )
    alpha = jnp.exp(m - m_new)
    p_pre = jnp.exp(s_pre - m_new)
    p_suf = jnp.where(mask, jnp.exp(s_suf - m_new), 0.0)
    l_new = alpha * l + (
        jnp.sum(p_pre, axis=1, keepdims=True) + jnp.sum(p_suf, axis=1, keepdims=True)
    )
    nt = (((1,), (1,)), ((), ()))
    pv = lax.dot_general(
        p_pre.astype(jnp.bfloat16), vt[:, :pre_len], nt, preferred_element_type=jnp.float32
    ) + lax.dot_general(
        p_suf.astype(jnp.bfloat16), vt[:, pre_len:], nt, preferred_element_type=jnp.float32
    )
    st_ref[:, :HD] = alpha * acc + pv
    st_ref[:, HD:HD + 1] = l_new
    st_ref[:, HD + 1:HD + 2] = m_new


def attention_block(q_heads, kv_blk, offset, scalars, state, pre_len):
    heads, rows, _ = q_heads.shape
    width = kv_blk.shape[1]
    kernel = lambda *refs: attn_kernel(*refs, pre_len=pre_len)
    st_spec = pl.BlockSpec((None, rows, state.shape[2]), lambda h: (h, 0, 0))
    return pl.pallas_call(
        kernel,
        grid=(heads,),
        in_specs=[
            pl.BlockSpec(memory_space=pltpu.SMEM),
            pl.BlockSpec(memory_space=pltpu.SMEM),
            pl.BlockSpec((None, rows, HD), lambda h: (h, 0, 0)),
            pl.BlockSpec((HD, width), lambda h: (h, 0)),
            pl.BlockSpec((HD, width), lambda h: (heads + h, 0)),
            st_spec,
        ],
        out_specs=st_spec,
        out_shape=jax.ShapeDtypeStruct(state.shape, jnp.float32),
        input_output_aliases={5: 0},
        cost_estimate=pl.CostEstimate(
            flops=4 * heads * rows * width * HD,
            transcendentals=heads * rows * width,
            bytes_accessed=2 * kv_blk.size + 8 * state.size,
        ),
        compiler_params=pltpu.CompilerParams(
            dimension_semantics=("arbitrary",), vmem_limit_bytes=63 * 1024 * 1024
        ),
    )(offset, scalars, q_heads, kv_blk, kv_blk, state)


def body(
    residual,
    queries,
    suffix_kv,
    prefix_kv,
    page_table,
    suffix_lens,
    w_out,
    norm_gain,
    w_gate,
    w_up,
    w_down,
):
    tok_rows = queries.shape[0]
    kv_width = KVH * HD
    per_group = QH // KVH
    tok_index = lax.axis_index("kv") * tok_rows + jnp.arange(tok_rows, dtype=jnp.int32)
    request_lens = suffix_lens[0]
    request_of, request_start = request_info(request_lens, tok_index)
    positions = PREFIX + tok_index - request_start
    rotated_q = rotate(queries.astype(jnp.float32).reshape(tok_rows, QH, HD), positions).astype(
        jnp.bfloat16
    )
    q_heads = (
        rotated_q.reshape(tok_rows, KVH, per_group, HD)
        .transpose(1, 2, 0, 3)
        .reshape(KVH, per_group * tok_rows, HD)
    )
    page_count = prefix_kv.shape[0]
    page_size = prefix_kv.shape[1]
    pre_len = page_count * page_size
    key_count = pre_len + tok_rows
    page_pos = (
        page_table[:, None] * page_size + jnp.arange(page_size, dtype=jnp.int32)[None, :]
    ).reshape(-1)
    key_pos = jnp.concatenate([page_pos, positions]).astype(jnp.float32)
    raw_t = jnp.concatenate(
        [prefix_kv.reshape(pre_len, 2 * kv_width), suffix_kv], axis=0
    ).T
    half_dim = HD // 2
    exponent = jnp.arange(half_dim, dtype=jnp.float32) * (2.0 / HD)
    inverse = jnp.exp(-exponent * math.log(THETA))
    angles = inverse[:, None] * key_pos[None, :]
    cosine = jnp.cos(angles)[None]
    sine_part = jnp.sin(angles)[None]
    halves = raw_t[:kv_width].astype(jnp.float32).reshape(KVH, 2, half_dim, key_count)
    first_half = halves[:, 0]
    second = halves[:, 1]
    keys_t = jnp.stack(
        [first_half * cosine - second * sine_part, second * cosine + first_half * sine_part],
        axis=1,
    ).astype(jnp.bfloat16)
    values_t = raw_t[kv_width:]
    local_t = jnp.concatenate([keys_t.reshape(kv_width, key_count), values_t], axis=0)
    request_ends = jnp.cumsum(request_lens)
    base_scalars = jnp.stack(
        [tok_index[0]]
        + [v for j in range(3) for v in (request_ends[j], request_lens[j])]
    ).astype(jnp.int32)
    rows = per_group * tok_rows
    state = jnp.zeros((KVH, rows, 128), jnp.float32).at[:, :, HD + 1].set(NEG)
    n_kv = lax.axis_size("kv")
    me = lax.axis_index("kv")

    def absorb_block(state, blk, owner):
        offset = jnp.reshape(owner * tok_rows, (1,)).astype(jnp.int32)
        return attention_block(q_heads, blk, offset, base_scalars, state, pre_len)

    cw_pairs = [(i, (i + 1) % n_kv) for i in range(n_kv)]
    ccw_pairs = [(i, (i - 1) % n_kv) for i in range(n_kv)]
    prev_state = state
    state = absorb_block(state, local_t, me)
    cw_blk = local_t
    ccw_blk = local_t
    for step in range(1, n_kv // 2 + 1):
        if step > 1:
            (cw_blk, ccw_blk), unused = lax.optimization_barrier(((cw_blk, ccw_blk), prev_state))
        prev_state = state
        cw_blk = lax.ppermute(cw_blk, "kv", cw_pairs)
        if step < n_kv - step:
            ccw_blk = lax.ppermute(ccw_blk, "kv", ccw_pairs)
        state = absorb_block(state, cw_blk, (me - step) % n_kv)
        if step < n_kv - step:
            state = absorb_block(state, ccw_blk, (me + step) % n_kv)
    out_heads = (state[:, :, :HD] / state[:, :, HD:HD + 1]).astype(jnp.bfloat16)
    attended = (
        out_heads.reshape(KVH, per_group, tok_rows, HD)
        .transpose(2, 0, 1, 3)
        .reshape(tok_rows, QH * HD)
    )
    mixed_sum = residual.astype(jnp.float32) + jnp.dot(
        attended, w_out, preferred_element_type=jnp.float32
    )
    stream_wide = mixed_sum.astype(jnp.bfloat16).astype(jnp.float32)
    normed = (
        stream_wide
        * lax.rsqrt(jnp.mean(stream_wide * stream_wide, axis=1, keepdims=True) + 1e-05)
        * norm_gain
    ).astype(jnp.bfloat16)
    shard_piece = lax.all_gather(normed, "req", axis=0, tiled=True)
    gate_proj = jnp.dot(shard_piece, w_gate, preferred_element_type=jnp.float32)
    up_proj = jnp.dot(shard_piece, w_up, preferred_element_type=jnp.float32)
    activated = (jax.nn.silu(gate_proj) * up_proj).astype(jnp.bfloat16)
    activated = lax.optimization_barrier(activated)
    summed = lax.psum_scatter(
        jnp.dot(activated, w_down, preferred_element_type=jnp.float32).astype(jnp.bfloat16),
        "req",
        scatter_dimension=0,
        tiled=True,
    ).astype(jnp.float32)
    layer_out = (stream_wide + summed).astype(jnp.bfloat16)
    return (attended, layer_out)


def solution(mesh):
    in_specs = (
        P(("req", "kv"), None),
        P(("req", "kv"), None),
        P(("req", "kv"), None),
        P("kv", None, None),
        P("kv"),
        P("req", None),
        P(),
        P(),
        P(None, "req"),
        P(None, "req"),
        P("req", None),
    )
    out_specs = (P(("req", "kv"), None), P(("req", "kv"), None))
    return jax.shard_map(body, mesh=mesh, in_specs=in_specs, out_specs=out_specs, check_vma=False)
```
